512 devices in a mesh: pipe: 16 (over y, x), seq: 32 (over z, core).
Axes of the slice: x: 4, y: 4, z: 16, core: 2. Of those that a mesh axis runs over, the one named last changes fastest.
Arguments:
- queries: bfloat16 [16, 2, 4096, 2048], P('pipe', None, 'seq'), may hold values from -120 to 120
- keys: bfloat16 [16, 2, 4096, 512], P('pipe', None, 'seq'), may hold values from -5 to 5
- values: bfloat16 [16, 2, 4096, 512], P('pipe', None, 'seq'), may hold values from -6 to 6
- out_grad: bfloat16 [2, 4096, 2048], P(None, 'seq'), may hold values from -6 to 6
- segments: int32 [2, 4096], replicated, may hold values from 0 to 63, never falling along the last dimension, each value on 1 to 256 neighbouring positions
Outputs:
- query_grads: bfloat16 [16, 2, 4096, 2048], P('pipe', None, 'seq')
- key_grads: bfloat16 [16, 2, 4096, 512], P('pipe', None, 'seq')
- value_grads: bfloat16 [16, 2, 4096, 512], P('pipe', None, 'seq')
The draws below stay inside these ranges and needn't reach their ends.
Inputs may be any that keep to these rules, and one draw needn't show every extreme that they name: `segments`: segment numbers never fall along a micro-batch.
All inputs are finite; a program needn't handle non-finite values.
Results may differ from the reference program's by a relative error of at most 0.014.
Values may be sent and summed in bfloat16 or wider, within the bound.
No kernel may reach another device: no remote copies, remote signals or barrier semaphores. Data moves between devices by JAX's collectives and lax.ppermute only.
A program may use at most 64 MiB of HBM per device.

```python
import math
import jax
import jax.numpy as jnp
import numpy as np
from jax import lax

TOK_DEV = 128
MICRO = 2
HQ = 16
HK = 4
DH = 128
WINDOW = 128
SECTIONS = 16
TOKENS = 4096
N_SEQ = 32


def drawn_pair(key):
    key_base = jnp.clip(jax.random.normal(jax.random.fold_in(key, 11), (SECTIONS, MICRO, TOKENS, HK, DH), jnp.float32), -5.0, 5.0)
    query_base = jnp.clip(jax.random.normal(jax.random.fold_in(key, 12), (SECTIONS, MICRO, TOKENS, HK, HQ // HK, DH), jnp.float32), -5.0, 5.0)
    return (query_base, key_base)


def draw_queries(key, part):
    query_mod, key_mod = drawn_pair(jax.random.fold_in(key, 5))
    return query_mod.reshape(SECTIONS, MICRO, TOKENS, HQ * DH).astype(jnp.bfloat16)


def draw_keys(key, part):
    query_mod, key_mod = drawn_pair(jax.random.fold_in(key, 5))
    return key_mod.reshape(SECTIONS, MICRO, TOKENS, HK * DH).astype(jnp.bfloat16)


def shard_levels(rng, extent, pieces, low, largest):
    def one(axis_at, shards_of):
        draws = jax.random.uniform(jax.random.fold_in(jax.random.fold_in(rng, 6), axis_at), (shards_of,), jnp.float32, low / len(pieces), largest / len(pieces))
        return jnp.repeat(jnp.exp(draws), extent[axis_at] // shards_of).reshape((-1,) + (1,) * (len(extent) - axis_at - 1))

    factor_of = one(*pieces[0])
    for cut in pieces[1:]:
        factor_of = factor_of * one(*cut)
    return factor_of


def length_profile(number_of, total, bound, slope):
    portions = [(1 << 20) // math.isqrt(rank ** slope) + 1 for rank in range(2, number_of + 1)]
    rest, given = total - bound - (number_of - 1), [1] * (number_of - 1)
    while rest > 0:
        movable = [i for i in range(number_of - 1) if given[i] < bound]
        mass, left = sum([portions[i] for i in movable]), rest
        for i in movable:
            addition = min(bound - given[i], max(1, left * portions[i] // mass), rest)
            given[i] = given[i] + addition
            rest = rest - addition
    return np.array([bound] + given)


def ragged_sizes(stream_key, count, total, bound, slope):
    if count == 2:
        one = jax.random.randint(stream_key, (), max(1, total - bound), min(bound, total - 1) + 1)
        return jnp.stack([one, total - one])
    sizes = jnp.asarray(length_profile(count, total, bound, slope), jnp.int32)
    twos = (count - 1) // 2
    donor, sink = sizes[1:1 + 2 * twos:2], sizes[2:2 + 2 * twos:2]
    slack = jnp.minimum(donor - 1, bound - sink)
    passed = jax.random.randint(jax.random.fold_in(stream_key, 1), (twos,), 0, 1 << 20) % (slack + 1)
    sizes = sizes.at[1:1 + 2 * twos:2].set(donor - passed).at[2:2 + 2 * twos:2].set(sink + passed)
    return sizes[jax.random.permutation(jax.random.fold_in(stream_key, 2), count)]


def bell_draw(rng, dims, deviation, limit, cuts=(), kind=jnp.bfloat16):
    loudness = shard_levels(rng, dims, cuts, -0.22, 0.18) if cuts else 1.0
    result = jax.random.normal(rng, dims, jnp.float32) * deviation * loudness
    return jnp.minimum(jnp.maximum(result, -limit), limit).astype(kind)


def setup_inputs(seed: int = 0) -> dict:
    key_of = jax.random.split(jax.random.key(seed), 6)
    queries = draw_queries(jax.random.fold_in(key_of[5], 71), 0)
    keys = draw_keys(jax.random.fold_in(key_of[5], 71), 0)
    values = bell_draw(key_of[2], (SECTIONS, MICRO, TOKENS, HK * DH), 1.0, 6.0, ((0, 16), (2, 32)))
    out_grad = bell_draw(key_of[3], (MICRO, TOKENS, HQ * DH), 1.0, 6.0, ((1, 32),))
    segments = jax.vmap(lambda own: jnp.searchsorted(jnp.cumsum(ragged_sizes(own, 2 * N_SEQ, TOKENS, 2 * TOK_DEV, 2)), jnp.arange(TOKENS), side="right"))(jax.random.split(key_of[4], MICRO)).reshape((MICRO, TOKENS)).astype(jnp.int32)
    return dict(queries=queries, keys=keys, values=values, out_grad=out_grad, segments=segments)


def tile_backward(query, key_rows, value_rows, grad_out, allowed):
    row_count = query.shape[0]
    key_count = key_rows.shape[0]
    kv_heads = key_rows.shape[1] // DH
    group_size = query.shape[1] // (kv_heads * DH)
    score_scale = DH ** -0.5
    query_heads = query.reshape(row_count, kv_heads, group_size, DH).astype(jnp.float32)
    grad_heads = grad_out.reshape(row_count, kv_heads, group_size, DH).astype(jnp.float32)
    key_heads = key_rows.reshape(key_count, kv_heads, DH).astype(jnp.float32)
    value_heads = value_rows.reshape(key_count, kv_heads, DH).astype(jnp.float32)
    scores = jnp.einsum("qhgd,khd->hgqk", query_heads, key_heads) * score_scale
    masked = jnp.where(allowed, scores, -jnp.inf)
    row_max = jnp.max(masked, axis=-1, keepdims=True)
    weights = jnp.exp(masked - row_max)
    probability = weights / jnp.sum(weights, axis=-1, keepdims=True)
    prob_low = lax.optimization_barrier(probability.astype(jnp.bfloat16)).astype(jnp.float32)
    output = jnp.einsum("hgqk,khd->qhgd", prob_low, value_heads)
    grad_prob = jnp.einsum("qhgd,khd->hgqk", grad_heads, value_heads)
    grad_dot = jnp.transpose(jnp.sum(grad_heads * output, axis=-1), (1, 2, 0))[..., None]
    grad_score = probability * (grad_prob - grad_dot)
    grad_score = lax.optimization_barrier(grad_score.astype(jnp.bfloat16)).astype(jnp.float32)
    query_grad = jnp.einsum("hgqk,khd->qhgd", grad_score, key_heads) * score_scale
    key_grad = jnp.einsum("hgqk,qhgd->khd", grad_score, query_heads) * score_scale
    value_grad = jnp.einsum("hgqk,qhgd->khd", prob_low, grad_heads)
    return query_grad.reshape(row_count, -1), key_grad.reshape(key_count, -1), value_grad.reshape(key_count, -1)


def make_mask(seg_padded, block_index, row_count):
    query_pos = block_index * row_count + jnp.arange(row_count, dtype=jnp.int32)
    key_pos = block_index * row_count - row_count + jnp.arange(2 * row_count, dtype=jnp.int32)
    seg_query = lax.dynamic_slice_in_dim(seg_padded, block_index * row_count + row_count, row_count)
    seg_key = lax.dynamic_slice_in_dim(seg_padded, block_index * row_count, 2 * row_count)
    near = (key_pos[None, :] <= query_pos[:, None]) & (query_pos[:, None] - key_pos[None, :] < WINDOW)
    return near & (key_pos[None, :] >= 0) & (seg_query[:, None] == seg_key[None, :])


def layer_backward(query_all, key_all, value_all, grad_all, seg_padded):
    row_count = TOK_DEV
    key_padded = jnp.concatenate([jnp.zeros((row_count, key_all.shape[1]), key_all.dtype), key_all], axis=0)
    value_padded = jnp.concatenate([jnp.zeros((row_count, value_all.shape[1]), value_all.dtype), value_all], axis=0)

    def block_grads(block_index):
        query = lax.dynamic_slice_in_dim(query_all, block_index * row_count, row_count)
        grad_out = lax.dynamic_slice_in_dim(grad_all, block_index * row_count, row_count)
        key_rows = lax.dynamic_slice_in_dim(key_padded, block_index * row_count, 2 * row_count)
        value_rows = lax.dynamic_slice_in_dim(value_padded, block_index * row_count, 2 * row_count)
        allowed = make_mask(seg_padded, block_index, row_count)
        return tile_backward(query, key_rows, value_rows, grad_out, allowed)

    query_grad, key_pair, value_pair = lax.map(block_grads, jnp.arange(N_SEQ, dtype=jnp.int32))

    def combine(pair):
        later = jnp.concatenate([pair[1:, :row_count], jnp.zeros_like(pair[:1, :row_count])], axis=0)
        return (pair[:, row_count:] + later).reshape(TOKENS, -1).astype(jnp.bfloat16)

    return query_grad.reshape(TOKENS, -1), combine(key_pair), combine(value_pair)


def reference(queries, keys, values, out_grad, segments):
    query_out = [[None] * MICRO for section_index in range(SECTIONS)]
    key_out = [[None] * MICRO for section_index in range(SECTIONS)]
    value_out = [[None] * MICRO for section_index in range(SECTIONS)]
    for batch_index in range(MICRO):
        seg_padded = jnp.concatenate([jnp.full((TOK_DEV,), -1, jnp.int32), segments[batch_index].astype(jnp.int32)])
        current = out_grad[batch_index]
        for section_index in reversed(range(SECTIONS)):
            query_grad, key_grad, value_grad = layer_backward(queries[section_index, batch_index], keys[section_index, batch_index], values[section_index, batch_index], current, seg_padded)
            current = (current.astype(jnp.float32) + query_grad).astype(jnp.bfloat16)
            query_out[section_index][batch_index] = current
            key_out[section_index][batch_index] = key_grad
            value_out[section_index][batch_index] = value_grad

    def stacked(nested):
        return jnp.stack([jnp.stack(inner) for inner in nested])

    return (stacked(query_out), stacked(key_out), stacked(value_out))
```

```python
import jax
import jax.numpy as jnp
from jax import lax
from jax.sharding import PartitionSpec as P

DH = 128
WINDOW = 128


def from_behind(block, axis, distance):
    devices = range(lax.axis_size(axis))
    route = [(i - distance, i) for i in devices if i - distance in devices]
    return lax.ppermute(block, axis, route)


def softmax_rows(scores, allowed):
    masked = jnp.where(allowed, scores, -jnp.inf)
    row_max = jnp.max(masked, axis=-1, keepdims=True)
    weights = jnp.exp(masked - row_max)
    return weights / jnp.sum(weights, axis=-1, keepdims=True)


def tile_backward(query, key_rows, value_rows, grad_out, allowed):
    row_count = query.shape[0]
    key_count = key_rows.shape[0]
    kv_heads = key_rows.shape[1] // DH
    group_size = query.shape[1] // (kv_heads * DH)
    score_scale = DH ** (-0.5)
    query_heads = query.reshape(row_count, kv_heads, group_size, DH)
    grad_heads = grad_out.reshape(row_count, kv_heads, group_size, DH)
    key_heads = key_rows.reshape(key_count, kv_heads, DH)
    value_heads = value_rows.reshape(key_count, kv_heads, DH)
    scores = (
        jnp.einsum("qhgd,khd->hgqk", query_heads, key_heads, preferred_element_type=jnp.float32)
        * score_scale
    )
    probability = softmax_rows(scores, allowed)
    prob_low = probability.astype(jnp.bfloat16)
    output = jnp.einsum("hgqk,khd->qhgd", prob_low, value_heads, preferred_element_type=jnp.float32)
    grad_prob = jnp.einsum(
        "qhgd,khd->hgqk", grad_heads, value_heads, preferred_element_type=jnp.float32
    )
    grad_dot = jnp.transpose(jnp.sum(grad_heads.astype(jnp.float32) * output, axis=-1), (1, 2, 0))[
        ..., None
    ]
    grad_score = (probability * (grad_prob - grad_dot)).astype(jnp.bfloat16)
    key_grad = (
        jnp.einsum("hgqk,qhgd->khd", grad_score, query_heads, preferred_element_type=jnp.float32)
        * score_scale
    )
    value_grad = jnp.einsum(
        "hgqk,qhgd->khd", prob_low, grad_heads, preferred_element_type=jnp.float32
    )
    return key_grad.reshape(key_count, -1), value_grad.reshape(key_count, -1)


def chain_backward(query_t, key_t, value_t, grad_top, allowed):
    layer_count, row_count, width = query_t.shape
    heads = width // DH
    score_scale = DH ** (-0.5)
    query_heads = query_t.reshape(layer_count, row_count, heads, DH)
    scores = (
        jnp.einsum("lqhd,lkd->lhqk", query_heads, key_t, preferred_element_type=jnp.float32)
        * score_scale
    )
    probability = softmax_rows(scores, allowed[None, None])
    prob_low = probability.astype(jnp.bfloat16)
    output = jnp.einsum("lhqk,lkd->lhqd", prob_low, value_t, preferred_element_type=jnp.float32)
    grad_start = jnp.transpose(grad_top.reshape(row_count, heads, DH), (1, 0, 2))

    def step(index, carry):
        grad, grads = carry
        layer = layer_count - 1 - index
        value_rows = lax.dynamic_index_in_dim(value_t, layer, 0, keepdims=False)
        key_rows = lax.dynamic_index_in_dim(key_t, layer, 0, keepdims=False)
        prob = lax.dynamic_index_in_dim(probability, layer, 0, keepdims=False)
        out = lax.dynamic_index_in_dim(output, layer, 0, keepdims=False)
        grad_prob = jnp.einsum("hqd,kd->hqk", grad, value_rows, preferred_element_type=jnp.float32)
        grad_dot = jnp.sum(grad.astype(jnp.float32) * out, axis=-1, keepdims=True)
        grad_score = (prob * (grad_prob - grad_dot)).astype(jnp.bfloat16)
        query_grad = (
            jnp.einsum("hqk,kd->hqd", grad_score, key_rows, preferred_element_type=jnp.float32)
            * score_scale
        )
        grad_next = (grad.astype(jnp.float32) + query_grad).astype(jnp.bfloat16)
        grads = lax.dynamic_update_index_in_dim(grads, grad_next, layer, 0)
        return grad_next, grads

    grads = jnp.zeros((layer_count, heads, row_count, DH), jnp.bfloat16)
    _, grads = lax.fori_loop(0, layer_count, step, (grad_start, grads))
    return jnp.transpose(grads, (0, 2, 1, 3)).reshape(layer_count, row_count, width)


def per_device(queries, keys, values, out_grad, segments):
    micro_count = queries.shape[1]
    row_count = queries.shape[2]
    query_width = queries.shape[3]
    key_width = keys.shape[3]
    section_count = lax.axis_size("pipe")
    section_index = lax.axis_index("pipe")
    seq_index = lax.axis_index("seq")
    kv_heads = key_width // DH
    q_heads = query_width // DH
    group_size = q_heads // kv_heads
    head_blocks = section_count // micro_count
    block_heads = q_heads // head_blocks
    block_width = block_heads * DH
    blocks_per_kv = group_size // block_heads
    own_query = queries[0]
    own_key = keys[0]
    own_value = values[0]
    seg_padded = jnp.concatenate(
        [jnp.full((micro_count, row_count), -1, jnp.int32), segments], axis=1
    )
    query_pos = seq_index * row_count + jnp.arange(row_count, dtype=jnp.int32)
    key_pos = seq_index * row_count - row_count + jnp.arange(2 * row_count, dtype=jnp.int32)
    seg_query = lax.dynamic_slice_in_dim(
        seg_padded, seq_index * row_count + row_count, row_count, axis=1
    )
    seg_key = lax.dynamic_slice_in_dim(seg_padded, seq_index * row_count, 2 * row_count, axis=1)
    near = (
        (key_pos[None, :] <= query_pos[:, None])
        & (query_pos[:, None] - key_pos[None, :] < WINDOW)
        & (key_pos[None, :] >= 0)
    )
    masks = near[None] & (seg_query[:, :, None] == seg_key[:, None, :])
    halo_key, halo_value = from_behind((own_key, own_value), "seq", 1)
    key_rows = jnp.concatenate([halo_key, own_key], axis=1)
    value_rows = jnp.concatenate([halo_value, own_value], axis=1)

    my_block = section_index // micro_count
    my_micro = section_index % micro_count
    my_kv = my_block // blocks_per_kv
    query_send = jnp.transpose(
        own_query.reshape(micro_count, row_count, head_blocks, block_width), (2, 0, 1, 3)
    ).reshape(section_count, row_count, block_width)
    kv_send = []
    for rows in (key_rows, value_rows):
        split = jnp.transpose(rows.reshape(micro_count, 2 * row_count, kv_heads, DH), (2, 0, 1, 3))
        split = jnp.broadcast_to(
            split[:, None], (kv_heads, blocks_per_kv, micro_count, 2 * row_count, DH)
        )
        kv_send.append(split.reshape(section_count, 2 * row_count, DH))
    query_t = lax.all_to_all(query_send, "pipe", 0, 0)
    key_t = lax.all_to_all(kv_send[0], "pipe", 0, 0)
    value_t = lax.all_to_all(kv_send[1], "pipe", 0, 0)
    grad_top = lax.dynamic_slice(
        out_grad, (my_micro, 0, my_block * block_width), (1, row_count, block_width)
    )[0]
    allowed = lax.dynamic_index_in_dim(masks, my_micro, 0, keepdims=False)
    grads = chain_backward(query_t, key_t, value_t, grad_top, allowed)
    grads_above = jnp.concatenate([grads[1:], grad_top[None]], axis=0)
    back_send = jnp.stack([grads_above, grads], axis=1)
    back = lax.all_to_all(back_send, "pipe", 0, 0)
    back = jnp.transpose(
        back.reshape(head_blocks, micro_count, 2, row_count, block_width), (2, 1, 3, 0, 4)
    ).reshape(2, micro_count, row_count, query_width)
    grad_in = back[0]
    query_all = back[1]

    key_parts = []
    value_parts = []
    for micro in range(micro_count):
        key_grad, value_grad = tile_backward(
            own_query[micro], key_rows[micro], value_rows[micro], grad_in[micro], masks[micro]
        )
        key_parts.append(key_grad)
        value_parts.append(value_grad)
    key_all = jnp.stack(key_parts)
    value_all = jnp.stack(value_parts)
    back_key, back_value = from_behind(
        (key_all[:, :row_count], value_all[:, :row_count]), "seq", -1
    )
    key_grads = (key_all[:, row_count:] + back_key).astype(jnp.bfloat16)
    value_grads = (value_all[:, row_count:] + back_value).astype(jnp.bfloat16)
    return (query_all[None], key_grads[None], value_grads[None])


def solution(mesh):
    placed = (
        P("pipe", None, "seq", None),
        P("pipe", None, "seq", None),
        P("pipe", None, "seq", None),
        P(None, "seq", None),
        P(),
    )
    return jax.shard_map(
        per_device,
        mesh=mesh,
        in_specs=placed,
        out_specs=(
            P("pipe", None, "seq", None),
            P("pipe", None, "seq", None),
            P("pipe", None, "seq", None),
        ),
        check_vma=False,
    )
```

```python
import jax
import jax.numpy as jnp
from jax import lax
from jax.experimental import pallas as pl
from jax.experimental.pallas import tpu as pltpu
from jax.sharding import PartitionSpec as P

DH = 128
WINDOW = 128
SCALE = DH ** (-0.5)
NT = (((1,), (1,)), ((), ()))
TN = (((0,), (0,)), ((), ()))


def from_behind(block, axis, distance):
    devices = range(lax.axis_size(axis))
    route = [(i - distance, i) for i in devices if i - distance in devices]
    return lax.ppermute(block, axis, route)


def head_core(q, k, v, g, allowed):
    scores = lax.dot_general(q, k, NT, preferred_element_type=jnp.float32) * SCALE
    masked = jnp.where(allowed, scores, -jnp.inf)
    row_max = jnp.max(masked, axis=-1, keepdims=True)
    weights = jnp.exp(masked - row_max)
    prob = weights / jnp.sum(weights, axis=-1, keepdims=True)
    prob_low = prob.astype(jnp.bfloat16)
    out = jnp.dot(prob_low, v, preferred_element_type=jnp.float32)
    grad_prob = lax.dot_general(g, v, NT, preferred_element_type=jnp.float32)
    grad_dot = jnp.sum(g.astype(jnp.float32) * out, axis=-1, keepdims=True)
    grad_score = (prob * (grad_prob - grad_dot)).astype(jnp.bfloat16)
    return prob_low, grad_score


def chain_kernel(q_ref, k_ref, v_ref, g0_ref, m_ref, o_ref):
    layers = q_ref.shape[0]
    heads = q_ref.shape[2] // DH
    allowed = m_ref[...] != 0

    def step(i, g):
        layer = layers - 1 - i
        k = k_ref[layer]
        v = v_ref[layer]
        outs = []
        for h in range(heads):
            cols = slice(h * DH, (h + 1) * DH)
            q = q_ref[layer, :, cols]
            gh = g[:, cols]
            _, grad_score = head_core(q, k, v, gh, allowed)
            dq = jnp.dot(grad_score, k, preferred_element_type=jnp.float32) * SCALE
            outs.append((gh.astype(jnp.float32) + dq).astype(jnp.bfloat16))
        g_new = jnp.concatenate(outs, axis=-1) if heads > 1 else outs[0]
        o_ref[layer] = g_new
        return g_new

    lax.fori_loop(0, layers, step, g0_ref[...])


def chain_call(query_t, key_t, value_t, grad_top, allowed_i32, interpret=False):
    return pl.pallas_call(
        chain_kernel,
        out_shape=jax.ShapeDtypeStruct(query_t.shape, jnp.bfloat16),
        interpret=interpret,
    )(query_t, key_t, value_t, grad_top, allowed_i32)


def layer_kernel(q_ref, k_ref, v_ref, g_ref, m_ref, dk_ref, dv_ref, gl_ref):
    heads = q_ref.shape[2] // DH
    allowed = m_ref[0] != 0
    k = k_ref[0]
    v = v_ref[0]
    dk = None
    dv = None
    for h in range(heads):
        cols = slice(h * DH, (h + 1) * DH)
        q = q_ref[0, :, cols]
        g = g_ref[0, :, cols]
        prob_low, grad_score = head_core(q, k, v, g, allowed)
        dq = jnp.dot(grad_score, k, preferred_element_type=jnp.float32) * SCALE
        gl_ref[0, :, cols] = (g.astype(jnp.float32) + dq).astype(jnp.bfloat16)
        dk_h = lax.dot_general(grad_score, q, TN, preferred_element_type=jnp.float32)
        dv_h = lax.dot_general(prob_low, g, TN, preferred_element_type=jnp.float32)
        dk = dk_h if dk is None else dk + dk_h
        dv = dv_h if dv is None else dv + dv_h
    dk_ref[0] = dk * SCALE
    dv_ref[0] = dv


def layer_call(query, key_rows, value_rows, grad_in, allowed_i32, interpret=False):
    micro, rows, width = query.shape
    keys2 = key_rows.shape[1]
    kv_heads = key_rows.shape[2] // DH
    group = width // (kv_heads * DH)
    gw = group * DH
    return pl.pallas_call(
        layer_kernel,
        grid=(micro, kv_heads),
        in_specs=[
            pl.BlockSpec((1, rows, gw), lambda m, g: (m, 0, g)),
            pl.BlockSpec((1, keys2, DH), lambda m, g: (m, 0, g)),
            pl.BlockSpec((1, keys2, DH), lambda m, g: (m, 0, g)),
            pl.BlockSpec((1, rows, gw), lambda m, g: (m, 0, g)),
            pl.BlockSpec((1, rows, keys2), lambda m, g: (m, 0, 0)),
        ],
        out_specs=[
            pl.BlockSpec((1, keys2, DH), lambda m, g: (m, 0, g)),
            pl.BlockSpec((1, keys2, DH), lambda m, g: (m, 0, g)),
            pl.BlockSpec((1, rows, gw), lambda m, g: (m, 0, g)),
        ],
        out_shape=[
            jax.ShapeDtypeStruct(key_rows.shape, jnp.float32),
            jax.ShapeDtypeStruct(key_rows.shape, jnp.float32),
            jax.ShapeDtypeStruct(query.shape, jnp.bfloat16),
        ],
        interpret=interpret,
    )(query, key_rows, value_rows, grad_in, allowed_i32)


def per_device(queries, keys, values, out_grad, segments):
    micro_count = queries.shape[1]
    row_count = queries.shape[2]
    query_width = queries.shape[3]
    key_width = keys.shape[3]
    section_count = lax.axis_size("pipe")
    section_index = lax.axis_index("pipe")
    seq_index = lax.axis_index("seq")
    kv_heads = key_width // DH
    q_heads = query_width // DH
    group_size = q_heads // kv_heads
    head_blocks = section_count // micro_count
    block_heads = q_heads // head_blocks
    block_width = block_heads * DH
    blocks_per_kv = group_size // block_heads
    own_query = queries[0]
    own_key = keys[0]
    own_value = values[0]
    seg_padded = jnp.concatenate(
        [jnp.full((micro_count, row_count), -1, jnp.int32), segments], axis=1
    )
    query_pos = seq_index * row_count + jnp.arange(row_count, dtype=jnp.int32)
    key_pos = seq_index * row_count - row_count + jnp.arange(2 * row_count, dtype=jnp.int32)
    seg_query = lax.dynamic_slice_in_dim(
        seg_padded, seq_index * row_count + row_count, row_count, axis=1
    )
    seg_key = lax.dynamic_slice_in_dim(seg_padded, seq_index * row_count, 2 * row_count, axis=1)
    near = (
        (key_pos[None, :] <= query_pos[:, None])
        & (query_pos[:, None] - key_pos[None, :] < WINDOW)
        & (key_pos[None, :] >= 0)
    )
    masks = (near[None] & (seg_query[:, :, None] == seg_key[:, None, :])).astype(jnp.int32)
    halo_key, halo_value = from_behind((own_key, own_value), "seq", 1)
    key_rows = jnp.concatenate([halo_key, own_key], axis=1)
    value_rows = jnp.concatenate([halo_value, own_value], axis=1)

    my_block = section_index // micro_count
    my_micro = section_index % micro_count
    query_send = jnp.transpose(
        own_query.reshape(micro_count, row_count, head_blocks, block_width), (2, 0, 1, 3)
    ).reshape(section_count, row_count, block_width)
    kv_send = []
    for rows in (own_key, own_value):
        split = jnp.transpose(rows.reshape(micro_count, row_count, kv_heads, DH), (2, 0, 1, 3))
        split = jnp.broadcast_to(
            split[:, None], (kv_heads, blocks_per_kv, micro_count, row_count, DH)
        )
        kv_send.append(split.reshape(section_count, row_count, DH))
    sent = lax.all_to_all(jnp.concatenate([query_send] + kv_send, axis=-1), "pipe", 0, 0)
    query_t = sent[..., :block_width]
    key_own_t = sent[..., block_width:block_width + DH]
    value_own_t = sent[..., block_width + DH:]
    key_halo_t, value_halo_t = from_behind((key_own_t, value_own_t), "seq", 1)
    key_t = jnp.concatenate([key_halo_t, key_own_t], axis=1)
    value_t = jnp.concatenate([value_halo_t, value_own_t], axis=1)
    grad_top = lax.dynamic_slice(
        out_grad, (my_micro, 0, my_block * block_width), (1, row_count, block_width)
    )[0]
    allowed = lax.dynamic_index_in_dim(masks, my_micro, 0, keepdims=False)
    grads = chain_call(query_t, key_t, value_t, grad_top, allowed)
    grads_above = jnp.concatenate([grads[1:], grad_top[None]], axis=0)
    back = lax.all_to_all(grads_above, "pipe", 0, 0)
    grad_in = jnp.transpose(
        back.reshape(head_blocks, micro_count, row_count, block_width), (1, 2, 0, 3)
    ).reshape(micro_count, row_count, query_width)

    key_all, value_all, query_all = layer_call(own_query, key_rows, value_rows, grad_in, masks)
    back_key, back_value = from_behind(
        (key_all[:, :row_count], value_all[:, :row_count]), "seq", -1
    )
    key_grads = (key_all[:, row_count:] + back_key).astype(jnp.bfloat16)
    value_grads = (value_all[:, row_count:] + back_value).astype(jnp.bfloat16)
    return (query_all[None], key_grads[None], value_grads[None])


def solution(mesh):
    placed = (
        P("pipe", None, "seq", None),
        P("pipe", None, "seq", None),
        P("pipe", None, "seq", None),
        P(None, "seq", None),
        P(),
    )
    return jax.shard_map(
        per_device,
        mesh=mesh,
        in_specs=placed,
        out_specs=(
            P("pipe", None, "seq", None),
            P("pipe", None, "seq", None),
            P("pipe", None, "seq", None),
        ),
        check_vma=False,
    )
```

```python
import jax
import jax.numpy as jnp
from jax import lax
from jax.experimental import pallas as pl
from jax.experimental.pallas import tpu as pltpu
from jax.sharding import PartitionSpec as P

DH = 128
WINDOW = 128
SCALE = DH ** (-0.5)
NT = (((1,), (1,)), ((), ()))
TN = (((0,), (0,)), ((), ()))


def from_behind(block, axis, distance):
    devices = range(lax.axis_size(axis))
    route = [(i - distance, i) for i in devices if i - distance in devices]
    return lax.ppermute(block, axis, route)


def head_core(q, k, v, g, allowed):
    scores = lax.dot_general(q, k, NT, preferred_element_type=jnp.float32) * SCALE
    masked = jnp.where(allowed, scores, -jnp.inf)
    row_max = jnp.max(masked, axis=-1, keepdims=True)
    weights = jnp.exp(masked - row_max)
    prob = weights / jnp.sum(weights, axis=-1, keepdims=True)
    prob_low = prob.astype(jnp.bfloat16)
    out = jnp.dot(prob_low, v, preferred_element_type=jnp.float32)
    grad_prob = lax.dot_general(g, v, NT, preferred_element_type=jnp.float32)
    grad_dot = jnp.sum(g.astype(jnp.float32) * out, axis=-1, keepdims=True)
    grad_score = (prob * (grad_prob - grad_dot)).astype(jnp.bfloat16)
    return prob_low, grad_score


def chain_kernel(x_ref, halo_ref, g0_ref, m_ref, o_ref):
    layers = x_ref.shape[0]
    width = o_ref.shape[2]
    heads = width // DH
    allowed = m_ref[...] != 0

    def step(i, g):
        layer = layers - 1 - i
        k = jnp.concatenate(
            [halo_ref[layer, :, :DH], x_ref[layer, :, width:width + DH]], axis=0
        )
        v = jnp.concatenate(
            [halo_ref[layer, :, DH:], x_ref[layer, :, width + DH:]], axis=0
        )
        outs = []
        for h in range(heads):
            cols = slice(h * DH, (h + 1) * DH)
            q = x_ref[layer, :, cols]
            gh = g[:, cols]
            _, grad_score = head_core(q, k, v, gh, allowed)
            dq = jnp.dot(grad_score, k, preferred_element_type=jnp.float32) * SCALE
            outs.append((gh.astype(jnp.float32) + dq).astype(jnp.bfloat16))
        g_new = jnp.concatenate(outs, axis=-1) if heads > 1 else outs[0]
        o_ref[layer] = g_new
        return g_new

    lax.fori_loop(0, layers, step, g0_ref[...], unroll=True)


def chain_call(sent, halo, grad_top, allowed_i32, interpret=False):
    layers, rows, _ = sent.shape
    return pl.pallas_call(
        chain_kernel,
        out_shape=jax.ShapeDtypeStruct((layers, rows, grad_top.shape[1]), jnp.bfloat16),
        interpret=interpret,
    )(sent, halo, grad_top, allowed_i32)


def layer_kernel(q_ref, kh_ref, ko_ref, vh_ref, vo_ref, g_ref, m_ref,
                 dkh_ref, dko_ref, dvh_ref, dvo_ref, gl_ref):
    heads = q_ref.shape[2] // DH
    rows = kh_ref.shape[1]
    allowed = m_ref[0] != 0
    k = jnp.concatenate([kh_ref[0], ko_ref[0]], axis=0)
    v = jnp.concatenate([vh_ref[0], vo_ref[0]], axis=0)
    dk = None
    dv = None
    for h in range(heads):
        cols = slice(h * DH, (h + 1) * DH)
        q = q_ref[0, :, cols]
        g = g_ref[0, :, cols]
        prob_low, grad_score = head_core(q, k, v, g, allowed)
        dq = jnp.dot(grad_score, k, preferred_element_type=jnp.float32) * SCALE
        gl_ref[0, :, cols] = (g.astype(jnp.float32) + dq).astype(jnp.bfloat16)
        dk_h = lax.dot_general(grad_score, q, TN, preferred_element_type=jnp.float32)
        dv_h = lax.dot_general(prob_low, g, TN, preferred_element_type=jnp.float32)
        dk = dk_h if dk is None else dk + dk_h
        dv = dv_h if dv is None else dv + dv_h
    dk = dk * SCALE
    dkh_ref[0] = dk[:rows]
    dko_ref[0] = dk[rows:]
    dvh_ref[0] = dv[:rows]
    dvo_ref[0] = dv[rows:]


def layer_call(query, key_halo, key_own, value_halo, value_own, grad_in, allowed_i32,
               interpret=False):
    micro, rows, width = query.shape
    kv_heads = key_own.shape[2] // DH
    group = width // (kv_heads * DH)
    gw = group * DH
    kv_spec = pl.BlockSpec((1, rows, DH), lambda m, g: (m, 0, g))
    q_spec = pl.BlockSpec((1, rows, gw), lambda m, g: (m, 0, g))
    kv_shape = jax.ShapeDtypeStruct(key_own.shape, jnp.float32)
    return pl.pallas_call(
        layer_kernel,
        grid=(micro, kv_heads),
        in_specs=[q_spec, kv_spec, kv_spec, kv_spec, kv_spec, q_spec,
                  pl.BlockSpec((1, rows, 2 * rows), lambda m, g: (m, 0, 0))],
        out_specs=[kv_spec, kv_spec, kv_spec, kv_spec, q_spec],
        out_shape=[kv_shape, kv_shape, kv_shape, kv_shape,
                   jax.ShapeDtypeStruct(query.shape, jnp.bfloat16)],
        interpret=interpret,
    )(query, key_halo, key_own, value_halo, value_own, grad_in, allowed_i32)


def per_device(queries, keys, values, out_grad, segments):
    micro_count = queries.shape[1]
    row_count = queries.shape[2]
    query_width = queries.shape[3]
    key_width = keys.shape[3]
    section_count = lax.axis_size("pipe")
    section_index = lax.axis_index("pipe")
    seq_index = lax.axis_index("seq")
    kv_heads = key_width // DH
    q_heads = query_width // DH
    group_size = q_heads // kv_heads
    head_blocks = section_count // micro_count
    block_heads = q_heads // head_blocks
    block_width = block_heads * DH
    blocks_per_kv = group_size // block_heads
    own_query = queries[0]
    own_key = keys[0]
    own_value = values[0]
    seg_padded = jnp.concatenate(
        [jnp.full((micro_count, row_count), -1, jnp.int32), segments], axis=1
    )
    query_pos = seq_index * row_count + jnp.arange(row_count, dtype=jnp.int32)
    key_pos = seq_index * row_count - row_count + jnp.arange(2 * row_count, dtype=jnp.int32)
    seg_query = lax.dynamic_slice_in_dim(
        seg_padded, seq_index * row_count + row_count, row_count, axis=1
    )
    seg_key = lax.dynamic_slice_in_dim(seg_padded, seq_index * row_count, 2 * row_count, axis=1)
    near = (
        (key_pos[None, :] <= query_pos[:, None])
        & (query_pos[:, None] - key_pos[None, :] < WINDOW)
        & (key_pos[None, :] >= 0)
    )
    masks = (near[None] & (seg_query[:, :, None] == seg_key[:, None, :])).astype(jnp.int32)
    halo_key, halo_value = from_behind((own_key, own_value), "seq", 1)

    my_block = section_index // micro_count
    my_micro = section_index % micro_count
    query_send = jnp.transpose(
        own_query.reshape(micro_count, row_count, head_blocks, block_width), (2, 0, 1, 3)
    ).reshape(section_count, row_count, block_width)
    kv_send = []
    for rows in (own_key, own_value):
        split = jnp.transpose(rows.reshape(micro_count, row_count, kv_heads, DH), (2, 0, 1, 3))
        split = jnp.broadcast_to(
            split[:, None], (kv_heads, blocks_per_kv, micro_count, row_count, DH)
        )
        kv_send.append(split.reshape(section_count, row_count, DH))
    sent = lax.all_to_all(jnp.concatenate([query_send] + kv_send, axis=-1), "pipe", 0, 0)
    sent, halo_key, halo_value = lax.optimization_barrier((sent, halo_key, halo_value))
    halo_t = from_behind(sent[..., block_width:], "seq", 1)
    grad_top = lax.dynamic_slice(
        out_grad, (my_micro, 0, my_block * block_width), (1, row_count, block_width)
    )[0]
    allowed = lax.dynamic_index_in_dim(masks, my_micro, 0, keepdims=False)
    grads = chain_call(sent, halo_t, grad_top, allowed)
    grads_above = jnp.concatenate([grads[1:], grad_top[None]], axis=0)
    back = lax.all_to_all(grads_above, "pipe", 0, 0)
    grad_in = jnp.transpose(
        back.reshape(head_blocks, micro_count, row_count, block_width), (1, 2, 0, 3)
    ).reshape(micro_count, row_count, query_width)

    key_back, key_own_grad, value_back, value_own_grad, query_all = layer_call(
        own_query, halo_key, own_key, halo_value, own_value, grad_in, masks
    )
    back_key, back_value = from_behind((key_back, value_back), "seq", -1)
    key_grads = (key_own_grad + back_key).astype(jnp.bfloat16)
    value_grads = (value_own_grad + back_value).astype(jnp.bfloat16)
    return (query_all[None], key_grads[None], value_grads[None])


def solution(mesh):
    placed = (
        P("pipe", None, "seq", None),
        P("pipe", None, "seq", None),
        P("pipe", None, "seq", None),
        P(None, "seq", None),
        P(),
    )
    return jax.shard_map(
        per_device,
        mesh=mesh,
        in_specs=placed,
        out_specs=(
            P("pipe", None, "seq", None),
            P("pipe", None, "seq", None),
            P("pipe", None, "seq", None),
        ),
        check_vma=False,
    )
```

```python
import functools

import jax
import jax.numpy as jnp
from jax import lax
from jax.experimental import pallas as pl
from jax.sharding import PartitionSpec as P


DH = 128
WINDOW = 128
SCALE = DH ** (-0.5)
NT = (((1,), (1,)), ((), ()))
TN = (((0,), (0,)), ((), ()))


def from_behind(block, axis, distance):
    devices = range(lax.axis_size(axis))
    route = [(i - distance, i) for i in devices if i - distance in devices]
    return lax.ppermute(block, axis, route)


def head_core(q, k, v, g, allowed):
    scores = lax.dot_general(q, k, NT, preferred_element_type=jnp.float32) * SCALE
    masked = jnp.where(allowed, scores, -jnp.inf)
    row_max = jnp.max(masked, axis=-1, keepdims=True)
    weights = jnp.exp(masked - row_max)
    prob = weights / jnp.sum(weights, axis=-1, keepdims=True)
    prob_low = prob.astype(jnp.bfloat16)
    out = jnp.dot(prob_low, v, preferred_element_type=jnp.float32)
    grad_prob = lax.dot_general(g, v, NT, preferred_element_type=jnp.float32)
    grad_dot = jnp.sum(g.astype(jnp.float32) * out, axis=-1, keepdims=True)
    grad_score = (prob * (grad_prob - grad_dot)).astype(jnp.bfloat16)
    return prob_low, grad_score


def chain_kernel(x_ref, halo_ref, g0_ref, m_ref, o_ref, g_out_ref, *, first):
    layers = halo_ref.shape[0]
    width = o_ref.shape[2]
    heads = width // DH
    allowed = m_ref[...] != 0

    def step(i, g):
        local = layers - 1 - i
        layer = first + local
        k = jnp.concatenate(
            [halo_ref[local, :, :DH], x_ref[layer, :, width:width + DH]], axis=0
        )
        v = jnp.concatenate(
            [halo_ref[local, :, DH:], x_ref[layer, :, width + DH:]], axis=0
        )
        outs = []
        for h in range(heads):
            cols = slice(h * DH, (h + 1) * DH)
            q = x_ref[layer, :, cols]
            gh = g[:, cols]
            _, grad_score = head_core(q, k, v, gh, allowed)
            dq = jnp.dot(grad_score, k, preferred_element_type=jnp.float32) * SCALE
            outs.append((gh.astype(jnp.float32) + dq).astype(jnp.bfloat16))
        g_new = jnp.concatenate(outs, axis=-1) if heads > 1 else outs[0]
        o_ref[local] = g_new
        return g_new

    g_out_ref[...] = lax.fori_loop(0, layers, step, g0_ref[...], unroll=True)


def chain_call(sent, halo, grad_top, allowed_i32, first, interpret=False):
    layers, rows, _ = halo.shape
    width = grad_top.shape[1]
    return pl.pallas_call(
        functools.partial(chain_kernel, first=first),
        out_shape=(
            jax.ShapeDtypeStruct((layers, rows, width), jnp.bfloat16),
            jax.ShapeDtypeStruct((rows, width), jnp.bfloat16),
        ),
        interpret=interpret,
    )(sent, halo, grad_top, allowed_i32)


def layer_kernel(q_ref, kh_ref, ko_ref, vh_ref, vo_ref, g_ref, m_ref,
                 dkh_ref, dko_ref, dvh_ref, dvo_ref, gl_ref):
    heads = q_ref.shape[2] // DH
    rows = kh_ref.shape[1]
    allowed = m_ref[0] != 0
    k = jnp.concatenate([kh_ref[0], ko_ref[0]], axis=0)
    v = jnp.concatenate([vh_ref[0], vo_ref[0]], axis=0)
    dk = None
    dv = None
    for h in range(heads):
        cols = slice(h * DH, (h + 1) * DH)
        q = q_ref[0, :, cols]
        g = g_ref[0, :, cols]
        prob_low, grad_score = head_core(q, k, v, g, allowed)
        dq = jnp.dot(grad_score, k, preferred_element_type=jnp.float32) * SCALE
        gl_ref[0, :, cols] = (g.astype(jnp.float32) + dq).astype(jnp.bfloat16)
        dk_h = lax.dot_general(grad_score, q, TN, preferred_element_type=jnp.float32)
        dv_h = lax.dot_general(prob_low, g, TN, preferred_element_type=jnp.float32)
        dk = dk_h if dk is None else dk + dk_h
        dv = dv_h if dv is None else dv + dv_h
    dk = dk * SCALE
    dkh_ref[0] = dk[:rows]
    dko_ref[0] = dk[rows:]
    dvh_ref[0] = dv[:rows]
    dvo_ref[0] = dv[rows:]


def layer_call(query, key_halo, key_own, value_halo, value_own, grad_in, allowed_i32, micro,
               interpret=False):
    _, rows, width = query.shape
    kv_heads = key_own.shape[2] // DH
    group = width // (kv_heads * DH)
    gw = group * DH
    kv_spec = pl.BlockSpec((1, rows, DH), lambda m, g: (micro, 0, g))
    q_spec = pl.BlockSpec((1, rows, gw), lambda m, g: (micro, 0, g))
    kv_out = pl.BlockSpec((1, rows, DH), lambda m, g: (0, 0, g))
    q_out = pl.BlockSpec((1, rows, gw), lambda m, g: (0, 0, g))
    kv_shape = jax.ShapeDtypeStruct((1, rows, key_own.shape[2]), jnp.float32)
    return pl.pallas_call(
        layer_kernel,
        grid=(1, kv_heads),
        in_specs=[q_spec, kv_spec, kv_spec, kv_spec, kv_spec, q_spec,
                  pl.BlockSpec((1, rows, 2 * rows), lambda m, g: (micro, 0, 0))],
        out_specs=[kv_out, kv_out, kv_out, kv_out, q_out],
        out_shape=[kv_shape, kv_shape, kv_shape, kv_shape,
                   jax.ShapeDtypeStruct((1, rows, width), jnp.bfloat16)],
        interpret=interpret,
    )(query, key_halo, key_own, value_halo, value_own, grad_in, allowed_i32)


def device_body(queries, keys, values, out_grad, segments):
    micro_count = queries.shape[1]
    row_count = queries.shape[2]
    query_width = queries.shape[3]
    key_width = keys.shape[3]
    section_count = lax.axis_size("pipe")
    section_index = lax.axis_index("pipe")
    seq_index = lax.axis_index("seq")
    kv_heads = key_width // DH
    q_heads = query_width // DH
    group_size = q_heads // kv_heads
    head_blocks = section_count // micro_count
    block_heads = q_heads // head_blocks
    block_width = block_heads * DH
    blocks_per_kv = group_size // block_heads
    own_query = queries[0]
    own_key = keys[0]
    own_value = values[0]
    seg_padded = jnp.concatenate(
        [jnp.full((micro_count, row_count), -1, jnp.int32), segments], axis=1
    )
    query_pos = seq_index * row_count + jnp.arange(row_count, dtype=jnp.int32)
    key_pos = seq_index * row_count - row_count + jnp.arange(2 * row_count, dtype=jnp.int32)
    seg_query = lax.dynamic_slice_in_dim(
        seg_padded, seq_index * row_count + row_count, row_count, axis=1
    )
    seg_key = lax.dynamic_slice_in_dim(seg_padded, seq_index * row_count, 2 * row_count, axis=1)
    near = (
        (key_pos[None, :] <= query_pos[:, None])
        & (query_pos[:, None] - key_pos[None, :] < WINDOW)
        & (key_pos[None, :] >= 0)
    )
    masks = (near[None] & (seg_query[:, :, None] == seg_key[:, None, :])).astype(jnp.int32)
    halo_key, halo_value = from_behind((own_key, own_value), "seq", 1)

    my_block = section_index // micro_count
    my_micro = section_index % micro_count
    query_send = jnp.transpose(
        own_query.reshape(micro_count, row_count, head_blocks, block_width), (2, 0, 1, 3)
    ).reshape(section_count, row_count, block_width)
    kv_send = []
    for rows in (own_key, own_value):
        split = jnp.transpose(rows.reshape(micro_count, row_count, kv_heads, DH), (2, 0, 1, 3))
        split = jnp.broadcast_to(
            split[:, None], (kv_heads, blocks_per_kv, micro_count, row_count, DH)
        )
        kv_send.append(split.reshape(section_count, row_count, DH))
    sent = lax.all_to_all(jnp.concatenate([query_send] + kv_send, axis=-1), "pipe", 0, 0)
    sent, halo_key, halo_value = lax.optimization_barrier((sent, halo_key, halo_value))
    split_at = section_count // 2
    halo_hi = from_behind(sent[split_at:, :, block_width:], "seq", 1)
    halo_lo = from_behind(sent[:split_at, :, block_width:], "seq", 1)
    grad_top = lax.dynamic_slice(
        out_grad, (my_micro, 0, my_block * block_width), (1, row_count, block_width)
    )[0]
    allowed = lax.dynamic_index_in_dim(masks, my_micro, 0, keepdims=False)
    grads_hi, grad_mid = chain_call(sent, halo_hi, grad_top, allowed, split_at)
    grads_lo, _ = chain_call(sent, halo_lo, grad_mid, allowed, 0)
    grads_above = jnp.concatenate([grads_lo[1:], grads_hi, grad_top[None]], axis=0)
    back = lax.all_to_all(grads_above, "pipe", 0, 0)
    grad_in = jnp.transpose(
        back.reshape(head_blocks, micro_count, row_count, block_width), (1, 2, 0, 3)
    ).reshape(micro_count, row_count, query_width)

    query_parts = []
    key_parts = []
    value_parts = []
    for micro in range(micro_count):
        key_back, key_own_grad, value_back, value_own_grad, query_part = layer_call(
            own_query, halo_key, own_key, halo_value, own_value, grad_in, masks, micro
        )
        back_key, back_value = from_behind(
            (key_back.astype(jnp.bfloat16), value_back.astype(jnp.bfloat16)), "seq", -1
        )
        key_parts.append(key_own_grad + back_key.astype(jnp.float32))
        value_parts.append(value_own_grad + back_value.astype(jnp.float32))
        query_parts.append(query_part)
    query_all = jnp.concatenate(query_parts, axis=0)
    key_grads = jnp.concatenate(key_parts, axis=0).astype(jnp.bfloat16)
    value_grads = jnp.concatenate(value_parts, axis=0).astype(jnp.bfloat16)
    return (query_all[None], key_grads[None], value_grads[None])


def solution(mesh):
    placed = (
        P("pipe", None, "seq", None),
        P("pipe", None, "seq", None),
        P("pipe", None, "seq", None),
        P(None, "seq", None),
        P(),
    )
    return jax.shard_map(
        device_body,
        mesh=mesh,
        in_specs=placed,
        out_specs=(
            P("pipe", None, "seq", None),
            P("pipe", None, "seq", None),
            P("pipe", None, "seq", None),
        ),
        check_vma=False,
    )
```

```python
import functools

import jax
import jax.numpy as jnp
from jax import lax
from jax.experimental import pallas as pl
from jax.sharding import PartitionSpec as P


DH = 128
WINDOW = 128
SCALE = DH ** (-0.5)
NT = (((1,), (1,)), ((), ()))
TN = (((0,), (0,)), ((), ()))


def from_behind(block, axis, distance):
    devices = range(lax.axis_size(axis))
    route = [(i - distance, i) for i in devices if i - distance in devices]
    return lax.ppermute(block, axis, route)


def head_core(q, k, v, g, allowed):
    scores = lax.dot_general(q, k, NT, preferred_element_type=jnp.float32) * SCALE
    masked = jnp.where(allowed, scores, -jnp.inf)
    row_max = jnp.max(masked, axis=-1, keepdims=True)
    weights = jnp.exp(masked - row_max)
    prob = weights / jnp.sum(weights, axis=-1, keepdims=True)
    prob_low = prob.astype(jnp.bfloat16)
    out = jnp.dot(prob_low, v, preferred_element_type=jnp.float32)
    grad_prob = lax.dot_general(g, v, NT, preferred_element_type=jnp.float32)
    grad_dot = jnp.sum(g.astype(jnp.float32) * out, axis=-1, keepdims=True)
    grad_score = (prob * (grad_prob - grad_dot)).astype(jnp.bfloat16)
    return prob_low, grad_score


def chain_kernel(x_ref, halo_ref, g0_ref, m_ref, o_ref, g_out_ref, *, first):
    layers = halo_ref.shape[0]
    width = o_ref.shape[2]
    heads = width // DH
    allowed = m_ref[...] != 0

    def step(i, g):
        local = layers - 1 - i
        layer = first + local
        k = jnp.concatenate(
            [halo_ref[local, :, :DH], x_ref[layer, :, width:width + DH]], axis=0
        )
        v = jnp.concatenate(
            [halo_ref[local, :, DH:], x_ref[layer, :, width + DH:]], axis=0
        )
        outs = []
        for h in range(heads):
            cols = slice(h * DH, (h + 1) * DH)
            q = x_ref[layer, :, cols]
            gh = g[:, cols]
            _, grad_score = head_core(q, k, v, gh, allowed)
            dq = jnp.dot(grad_score, k, preferred_element_type=jnp.float32) * SCALE
            outs.append((gh.astype(jnp.float32) + dq).astype(jnp.bfloat16))
        g_new = jnp.concatenate(outs, axis=-1) if heads > 1 else outs[0]
        o_ref[local] = g_new
        return g_new

    g_out_ref[...] = lax.fori_loop(0, layers, step, g0_ref[...], unroll=True)


def chain_call(sent, halo, grad_top, allowed_i32, first, interpret=False):
    layers, rows, _ = halo.shape
    width = grad_top.shape[1]
    return pl.pallas_call(
        functools.partial(chain_kernel, first=first),
        out_shape=(
            jax.ShapeDtypeStruct((layers, rows, width), jnp.bfloat16),
            jax.ShapeDtypeStruct((rows, width), jnp.bfloat16),
        ),
        interpret=interpret,
    )(sent, halo, grad_top, allowed_i32)


def layer_kernel(q_ref, kvo_ref, kvh_ref, ga_ref, gb_ref, m_ref, gi_ref,
                 dk_ref, dv_ref, back_ref, gl_ref):
    del gi_ref
    heads = q_ref.shape[3] // DH
    rows = q_ref.shape[2]
    allowed = m_ref[0] != 0
    k = jnp.concatenate([kvh_ref[0, 0, 0], kvo_ref[0, 0, 0]], axis=0)
    v = jnp.concatenate([kvh_ref[1, 0, 0], kvo_ref[1, 0, 0]], axis=0)
    grad = jnp.concatenate([ga_ref[0], gb_ref[0]], axis=-1)
    dk = None
    dv = None
    for h in range(heads):
        cols = slice(h * DH, (h + 1) * DH)
        q = q_ref[0, 0, :, cols]
        g = grad[:, cols]
        prob_low, grad_score = head_core(q, k, v, g, allowed)
        dq = jnp.dot(grad_score, k, preferred_element_type=jnp.float32) * SCALE
        gl_ref[0, 0, :, cols] = (g.astype(jnp.float32) + dq).astype(jnp.bfloat16)
        dk_h = lax.dot_general(grad_score, q, TN, preferred_element_type=jnp.float32)
        dv_h = lax.dot_general(prob_low, g, TN, preferred_element_type=jnp.float32)
        dk = dk_h if dk is None else dk + dk_h
        dv = dv_h if dv is None else dv + dv_h
    dk = dk * SCALE
    back_ref[0, 0] = dk[:rows].astype(back_ref.dtype)
    back_ref[1, 0] = dv[:rows].astype(back_ref.dtype)
    dk_ref[0] = dk[rows:]
    dv_ref[0] = dv[rows:]


def layer_call(queries, kv_own, kv_halo, grad_t, allowed_i32, grad_prev, micro,
               blocks_per_kv, interpret=False):
    _, micro_count, rows, width = queries.shape
    kv_heads = kv_own.shape[4] // DH
    group = width // (kv_heads * DH)
    gw = group * DH
    bw = grad_t.shape[2]
    kv_spec = pl.BlockSpec((2, 1, 1, rows, DH), lambda i, g: (0, 0, micro, 0, g))
    q_spec = pl.BlockSpec((1, 1, rows, gw), lambda i, g: (0, micro, 0, g))
    ga_spec = pl.BlockSpec(
        (1, rows, bw), lambda i, g: ((g * blocks_per_kv) * micro_count + micro, 0, 0))
    gb_spec = pl.BlockSpec(
        (1, rows, bw), lambda i, g: ((g * blocks_per_kv + 1) * micro_count + micro, 0, 0))
    own_out = pl.BlockSpec((1, rows, DH), lambda i, g: (0, 0, g))
    own_shape = jax.ShapeDtypeStruct((1, rows, kv_heads * DH), jnp.float32)
    return pl.pallas_call(
        layer_kernel,
        grid=(1, kv_heads),
        in_specs=[q_spec, kv_spec, kv_spec, ga_spec, gb_spec,
                  pl.BlockSpec((1, rows, 2 * rows), lambda i, g: (micro, 0, 0)),
                  pl.BlockSpec(memory_space=pl.ANY)],
        out_specs=[own_out, own_out,
                   pl.BlockSpec((2, 1, rows, DH), lambda i, g: (0, 0, 0, g)),
                   q_spec],
        out_shape=[own_shape, own_shape,
                   jax.ShapeDtypeStruct((2, 1, rows, kv_heads * DH), jnp.bfloat16),
                   jax.ShapeDtypeStruct(queries.shape, jnp.bfloat16)],
        input_output_aliases={6: 3},
        interpret=interpret,
    )(queries, kv_own, kv_halo, grad_t, grad_t, allowed_i32, grad_prev)


def device_body(queries, keys, values, out_grad, segments):
    micro_count = queries.shape[1]
    row_count = queries.shape[2]
    query_width = queries.shape[3]
    key_width = keys.shape[3]
    section_count = lax.axis_size("pipe")
    section_index = lax.axis_index("pipe")
    seq_index = lax.axis_index("seq")
    kv_heads = key_width // DH
    q_heads = query_width // DH
    group_size = q_heads // kv_heads
    head_blocks = section_count // micro_count
    block_heads = q_heads // head_blocks
    block_width = block_heads * DH
    blocks_per_kv = group_size // block_heads
    own_query = queries[0]
    own_key = keys[0]
    own_value = values[0]
    kv_own = jnp.stack([keys, values])
    seg_padded = jnp.concatenate(
        [jnp.full((micro_count, row_count), -1, jnp.int32), segments], axis=1
    )
    query_pos = seq_index * row_count + jnp.arange(row_count, dtype=jnp.int32)
    key_pos = seq_index * row_count - row_count + jnp.arange(2 * row_count, dtype=jnp.int32)
    seg_query = lax.dynamic_slice_in_dim(
        seg_padded, seq_index * row_count + row_count, row_count, axis=1
    )
    seg_key = lax.dynamic_slice_in_dim(seg_padded, seq_index * row_count, 2 * row_count, axis=1)
    near = (
        (key_pos[None, :] <= query_pos[:, None])
        & (query_pos[:, None] - key_pos[None, :] < WINDOW)
        & (key_pos[None, :] >= 0)
    )
    masks = (near[None] & (seg_query[:, :, None] == seg_key[:, None, :])).astype(jnp.int32)
    kv_halo = from_behind(kv_own, "seq", 1)

    my_block = section_index // micro_count
    my_micro = section_index % micro_count
    query_send = jnp.transpose(
        own_query.reshape(micro_count, row_count, head_blocks, block_width), (2, 0, 1, 3)
    ).reshape(section_count, row_count, block_width)
    kv_send = []
    for rows in (own_key, own_value):
        split = jnp.transpose(rows.reshape(micro_count, row_count, kv_heads, DH), (2, 0, 1, 3))
        split = jnp.broadcast_to(
            split[:, None], (kv_heads, blocks_per_kv, micro_count, row_count, DH)
        )
        kv_send.append(split.reshape(section_count, row_count, DH))
    sent = lax.all_to_all(jnp.concatenate([query_send] + kv_send, axis=-1), "pipe", 0, 0)
    sent, kv_halo = lax.optimization_barrier((sent, kv_halo))
    split_at = section_count // 2
    halo_hi = from_behind(sent[split_at:, :, block_width:], "seq", 1)
    halo_lo = from_behind(sent[:split_at, :, block_width:], "seq", 1)
    grad_top = lax.dynamic_slice(
        out_grad, (my_micro, 0, my_block * block_width), (1, row_count, block_width)
    )[0]
    allowed = lax.dynamic_index_in_dim(masks, my_micro, 0, keepdims=False)
    grads_hi, grad_mid = chain_call(sent, halo_hi, grad_top, allowed, split_at)
    grads_lo, _ = chain_call(sent, halo_lo, grad_mid, allowed, 0)
    grads_above = jnp.concatenate([grads_lo[1:], grads_hi, grad_top[None]], axis=0)
    grad_t = lax.all_to_all(grads_above, "pipe", 0, 0)

    query_all = jnp.zeros(queries.shape, jnp.bfloat16)
    key_parts = []
    value_parts = []
    for micro in range(micro_count):
        key_own_grad, value_own_grad, kv_back, query_all = layer_call(
            queries, kv_own, kv_halo, grad_t, masks, query_all, micro, blocks_per_kv
        )
        kv_next = from_behind(kv_back, "seq", -1)
        key_parts.append(key_own_grad + kv_next[0].astype(jnp.float32))
        value_parts.append(value_own_grad + kv_next[1].astype(jnp.float32))
    query_all = query_all[0]
    key_grads = jnp.concatenate(key_parts, axis=0).astype(jnp.bfloat16)
    value_grads = jnp.concatenate(value_parts, axis=0).astype(jnp.bfloat16)
    return (query_all[None], key_grads[None], value_grads[None])


def solution(mesh):
    placed = (
        P("pipe", None, "seq", None),
        P("pipe", None, "seq", None),
        P("pipe", None, "seq", None),
        P(None, "seq", None),
        P(),
    )
    return jax.shard_map(
        device_body,
        mesh=mesh,
        in_specs=placed,
        out_specs=(
            P("pipe", None, "seq", None),
            P("pipe", None, "seq", None),
            P("pipe", None, "seq", None),
        ),
        check_vma=False,
    )
```

```python
import functools

import jax
import jax.numpy as jnp
from jax import lax
from jax.experimental import pallas as pl
from jax.sharding import PartitionSpec as P


DH = 128
WINDOW = 128
SCALE = DH ** (-0.5)
NT = (((1,), (1,)), ((), ()))
TN = (((0,), (0,)), ((), ()))


def from_behind(block, axis, distance):
    devices = range(lax.axis_size(axis))
    route = [(i - distance, i) for i in devices if i - distance in devices]
    return lax.ppermute(block, axis, route)


def head_core(q, k, v, g, allowed):
    scores = lax.dot_general(q, k, NT, preferred_element_type=jnp.float32) * SCALE
    masked = jnp.where(allowed, scores, -jnp.inf)
    row_max = jnp.max(masked, axis=-1, keepdims=True)
    weights = jnp.exp(masked - row_max)
    prob = weights / jnp.sum(weights, axis=-1, keepdims=True)
    prob_low = prob.astype(jnp.bfloat16)
    out = jnp.dot(prob_low, v, preferred_element_type=jnp.float32)
    grad_prob = lax.dot_general(g, v, NT, preferred_element_type=jnp.float32)
    grad_dot = jnp.sum(g.astype(jnp.float32) * out, axis=-1, keepdims=True)
    grad_score = (prob * (grad_prob - grad_dot)).astype(jnp.bfloat16)
    return prob_low, grad_score


def chain_kernel(x_ref, halo_ref, g0_ref, m_ref, o_ref, g_out_ref, *, first):
    layers = halo_ref.shape[0]
    width = o_ref.shape[2]
    heads = width // DH
    allowed = m_ref[...] != 0

    def step(i, g):
        local = layers - 1 - i
        layer = first + local
        k = jnp.concatenate(
            [halo_ref[local, :, :DH], x_ref[layer, :, width:width + DH]], axis=0
        )
        v = jnp.concatenate(
            [halo_ref[local, :, DH:], x_ref[layer, :, width + DH:]], axis=0
        )
        outs = []
        for h in range(heads):
            cols = slice(h * DH, (h + 1) * DH)
            q = x_ref[layer, :, cols]
            gh = g[:, cols]
            _, grad_score = head_core(q, k, v, gh, allowed)
            dq = jnp.dot(grad_score, k, preferred_element_type=jnp.float32) * SCALE
            outs.append((gh.astype(jnp.float32) + dq).astype(jnp.bfloat16))
        g_new = jnp.concatenate(outs, axis=-1) if heads > 1 else outs[0]
        o_ref[local] = g_new
        return g_new

    g_out_ref[...] = lax.fori_loop(0, layers, step, g0_ref[...], unroll=True)


def chain_call(sent, halo, grad_top, allowed_i32, first, interpret=False):
    layers, rows, _ = halo.shape
    width = grad_top.shape[1]
    return pl.pallas_call(
        functools.partial(chain_kernel, first=first),
        out_shape=(
            jax.ShapeDtypeStruct((layers, rows, width), jnp.bfloat16),
            jax.ShapeDtypeStruct((rows, width), jnp.bfloat16),
        ),
        interpret=interpret,
    )(sent, halo, grad_top, allowed_i32)


def layer_pre_kernel(q_ref, kvo_ref, kvh_ref, m_ref, p_ref, o_ref):
    heads = q_ref.shape[3] // DH
    allowed = m_ref[0] != 0
    k = jnp.concatenate([kvh_ref[0, 0, 0], kvo_ref[0, 0, 0]], axis=0)
    v = jnp.concatenate([kvh_ref[1, 0, 0], kvo_ref[1, 0, 0]], axis=0)
    for h in range(heads):
        q = q_ref[0, 0, :, h * DH:(h + 1) * DH]
        scores = lax.dot_general(q, k, NT, preferred_element_type=jnp.float32) * SCALE
        masked = jnp.where(allowed, scores, -jnp.inf)
        row_max = jnp.max(masked, axis=-1, keepdims=True)
        weights = jnp.exp(masked - row_max)
        prob = weights / jnp.sum(weights, axis=-1, keepdims=True)
        p_ref[0, h] = prob
        o_ref[0, h] = jnp.dot(prob.astype(jnp.bfloat16), v, preferred_element_type=jnp.float32)


def layer_pre_call(queries, kv_own, kv_halo, allowed_i32, interpret=False):
    _, micro_count, rows, width = queries.shape
    kv_heads = kv_own.shape[4] // DH
    group = width // (kv_heads * DH)
    kv_spec = pl.BlockSpec((2, 1, 1, rows, DH), lambda m, g: (0, 0, m, 0, g))
    return pl.pallas_call(
        layer_pre_kernel,
        grid=(micro_count, kv_heads),
        in_specs=[pl.BlockSpec((1, 1, rows, group * DH), lambda m, g: (0, m, 0, g)),
                  kv_spec, kv_spec,
                  pl.BlockSpec((1, rows, 2 * rows), lambda m, g: (m, 0, 0))],
        out_specs=[pl.BlockSpec((1, group, rows, 2 * rows), lambda m, g: (m, g, 0, 0)),
                   pl.BlockSpec((1, group, rows, DH), lambda m, g: (m, g, 0, 0))],
        out_shape=[
            jax.ShapeDtypeStruct((micro_count, kv_heads * group, rows, 2 * rows), jnp.float32),
            jax.ShapeDtypeStruct((micro_count, kv_heads * group, rows, DH), jnp.float32),
        ],
        interpret=interpret,
    )(queries, kv_own, kv_halo, allowed_i32)


def layer_kernel(q_ref, kvo_ref, kvh_ref, ga_ref, gb_ref, p_ref, o_ref, *rest):
    dk_ref, dv_ref, back_ref, gl_ref = rest[-4:]
    heads = q_ref.shape[3] // DH
    rows = q_ref.shape[2]
    k = jnp.concatenate([kvh_ref[0, 0, 0], kvo_ref[0, 0, 0]], axis=0)
    v = jnp.concatenate([kvh_ref[1, 0, 0], kvo_ref[1, 0, 0]], axis=0)
    grad = jnp.concatenate([ga_ref[0], gb_ref[0]], axis=-1)
    dk = None
    dv = None
    for h in range(heads):
        cols = slice(h * DH, (h + 1) * DH)
        q = q_ref[0, 0, :, cols]
        g = grad[:, cols]
        prob = p_ref[0, h]
        prob_low = prob.astype(jnp.bfloat16)
        grad_prob = lax.dot_general(g, v, NT, preferred_element_type=jnp.float32)
        grad_dot = jnp.sum(g.astype(jnp.float32) * o_ref[0, h], axis=-1, keepdims=True)
        grad_score = (prob * (grad_prob - grad_dot)).astype(jnp.bfloat16)
        dq = jnp.dot(grad_score, k, preferred_element_type=jnp.float32) * SCALE
        gl_ref[0, 0, :, cols] = (g.astype(jnp.float32) + dq).astype(jnp.bfloat16)
        dk_h = lax.dot_general(grad_score, q, TN, preferred_element_type=jnp.float32)
        dv_h = lax.dot_general(prob_low, g, TN, preferred_element_type=jnp.float32)
        dk = dk_h if dk is None else dk + dk_h
        dv = dv_h if dv is None else dv + dv_h
    dk = dk * SCALE
    back_ref[0, 0] = dk[:rows].astype(back_ref.dtype)
    back_ref[1, 0] = dv[:rows].astype(back_ref.dtype)
    dk_ref[0] = dk[rows:]
    dv_ref[0] = dv[rows:]


def layer_call(queries, kv_own, kv_halo, grad_t, prob, out, grad_prev, micro,
               blocks_per_kv, interpret=False):
    _, micro_count, rows, width = queries.shape
    kv_heads = kv_own.shape[4] // DH
    group = width // (kv_heads * DH)
    gw = group * DH
    bw = grad_t.shape[2]
    kv_spec = pl.BlockSpec((2, 1, 1, rows, DH), lambda i, g: (0, 0, micro, 0, g))
    q_spec = pl.BlockSpec((1, 1, rows, gw), lambda i, g: (0, micro, 0, g))
    ga_spec = pl.BlockSpec(
        (1, rows, bw), lambda i, g: ((g * blocks_per_kv) * micro_count + micro, 0, 0))
    gb_spec = pl.BlockSpec(
        (1, rows, bw), lambda i, g: ((g * blocks_per_kv + 1) * micro_count + micro, 0, 0))
    p_spec = pl.BlockSpec((1, group, rows, 2 * rows), lambda i, g: (micro, g, 0, 0))
    o_spec = pl.BlockSpec((1, group, rows, DH), lambda i, g: (micro, g, 0, 0))
    own_out = pl.BlockSpec((1, rows, DH), lambda i, g: (0, 0, g))
    own_shape = jax.ShapeDtypeStruct((1, rows, kv_heads * DH), jnp.float32)
    in_specs = [q_spec, kv_spec, kv_spec, ga_spec, gb_spec, p_spec, o_spec]
    operands = [queries, kv_own, kv_halo, grad_t, grad_t, prob, out]
    aliases = {}
    if grad_prev is not None:
        in_specs.append(pl.BlockSpec(memory_space=pl.ANY))
        operands.append(grad_prev)
        aliases = {len(operands) - 1: 3}
    return pl.pallas_call(
        layer_kernel,
        grid=(1, kv_heads),
        in_specs=in_specs,
        out_specs=[own_out, own_out,
                   pl.BlockSpec((2, 1, rows, DH), lambda i, g: (0, 0, 0, g)),
                   q_spec],
        out_shape=[own_shape, own_shape,
                   jax.ShapeDtypeStruct((2, 1, rows, kv_heads * DH), jnp.bfloat16),
                   jax.ShapeDtypeStruct(queries.shape, jnp.bfloat16)],
        input_output_aliases=aliases,
        interpret=interpret,
    )(*operands)


def device_body(queries, keys, values, out_grad, segments):
    micro_count = queries.shape[1]
    row_count = queries.shape[2]
    query_width = queries.shape[3]
    key_width = keys.shape[3]
    section_count = lax.axis_size("pipe")
    section_index = lax.axis_index("pipe")
    seq_index = lax.axis_index("seq")
    kv_heads = key_width // DH
    q_heads = query_width // DH
    group_size = q_heads // kv_heads
    head_blocks = section_count // micro_count
    block_heads = q_heads // head_blocks
    block_width = block_heads * DH
    blocks_per_kv = group_size // block_heads
    own_query = queries[0]
    own_key = keys[0]
    own_value = values[0]
    kv_own = jnp.stack([keys, values])
    seg_padded = jnp.concatenate(
        [jnp.full((micro_count, row_count), -1, jnp.int32), segments], axis=1
    )
    query_pos = seq_index * row_count + jnp.arange(row_count, dtype=jnp.int32)
    key_pos = seq_index * row_count - row_count + jnp.arange(2 * row_count, dtype=jnp.int32)
    seg_query = lax.dynamic_slice_in_dim(
        seg_padded, seq_index * row_count + row_count, row_count, axis=1
    )
    seg_key = lax.dynamic_slice_in_dim(seg_padded, seq_index * row_count, 2 * row_count, axis=1)
    near = (
        (key_pos[None, :] <= query_pos[:, None])
        & (query_pos[:, None] - key_pos[None, :] < WINDOW)
        & (key_pos[None, :] >= 0)
    )
    masks = (near[None] & (seg_query[:, :, None] == seg_key[:, None, :])).astype(jnp.int32)
    kv_halo = from_behind(kv_own, "seq", 1)

    my_block = section_index // micro_count
    my_micro = section_index % micro_count
    query_send = jnp.transpose(
        own_query.reshape(micro_count, row_count, head_blocks, block_width), (2, 0, 1, 3)
    ).reshape(section_count, row_count, block_width)
    kv_send = []
    for rows in (own_key, own_value):
        split = jnp.transpose(rows.reshape(micro_count, row_count, kv_heads, DH), (2, 0, 1, 3))
        split = jnp.broadcast_to(
            split[:, None], (kv_heads, blocks_per_kv, micro_count, row_count, DH)
        )
        kv_send.append(split.reshape(section_count, row_count, DH))
    sent = lax.all_to_all(jnp.concatenate([query_send] + kv_send, axis=-1), "pipe", 0, 0)
    prob, out = layer_pre_call(queries, kv_own, kv_halo, masks)
    split_at = section_count // 2
    halo_hi = from_behind(sent[split_at:, :, block_width:], "seq", 1)
    halo_lo = from_behind(sent[:split_at, :, block_width:], "seq", 1)
    grad_top = lax.dynamic_slice(
        out_grad, (my_micro, 0, my_block * block_width), (1, row_count, block_width)
    )[0]
    allowed = lax.dynamic_index_in_dim(masks, my_micro, 0, keepdims=False)
    grads_hi, grad_mid = chain_call(sent, halo_hi, grad_top, allowed, split_at)
    grads_lo, _ = chain_call(sent, halo_lo, grad_mid, allowed, 0)
    grads_above = jnp.concatenate([grads_lo[1:], grads_hi, grad_top[None]], axis=0)
    grad_t = lax.all_to_all(grads_above, "pipe", 0, 0)

    query_all = None
    key_parts = []
    value_parts = []
    for micro in range(micro_count):
        key_own_grad, value_own_grad, kv_back, query_all = layer_call(
            queries, kv_own, kv_halo, grad_t, prob, out, query_all, micro, blocks_per_kv
        )
        kv_next = from_behind(kv_back, "seq", -1)
        key_parts.append(key_own_grad + kv_next[0].astype(jnp.float32))
        value_parts.append(value_own_grad + kv_next[1].astype(jnp.float32))
    query_all = query_all[0]
    key_grads = jnp.concatenate(key_parts, axis=0).astype(jnp.bfloat16)
    value_grads = jnp.concatenate(value_parts, axis=0).astype(jnp.bfloat16)
    return (query_all[None], key_grads[None], value_grads[None])


def solution(mesh):
    placed = (
        P("pipe", None, "seq", None),
        P("pipe", None, "seq", None),
        P("pipe", None, "seq", None),
        P(None, "seq", None),
        P(),
    )
    return jax.shard_map(
        device_body,
        mesh=mesh,
        in_specs=placed,
        out_specs=(
            P("pipe", None, "seq", None),
            P("pipe", None, "seq", None),
            P("pipe", None, "seq", None),
        ),
        check_vma=False,
    )
```

```python
import functools

import jax
import jax.numpy as jnp
from jax import lax
from jax.experimental import pallas as pl
from jax.sharding import PartitionSpec as P


DH = 128
WINDOW = 128
SCALE = DH ** (-0.5)
NT = (((1,), (1,)), ((), ()))
TN = (((0,), (0,)), ((), ()))


def from_behind(block, axis, distance):
    devices = range(lax.axis_size(axis))
    route = [(i - distance, i) for i in devices if i - distance in devices]
    return lax.ppermute(block, axis, route)


def head_core(q, k, v, g, allowed):
    scores = lax.dot_general(q, k, NT, preferred_element_type=jnp.float32) * SCALE
    masked = jnp.where(allowed, scores, -jnp.inf)
    row_max = jnp.max(masked, axis=-1, keepdims=True)
    weights = jnp.exp(masked - row_max)
    prob = weights / jnp.sum(weights, axis=-1, keepdims=True)
    prob_low = prob.astype(jnp.bfloat16)
    out = jnp.dot(prob_low, v, preferred_element_type=jnp.float32)
    grad_prob = lax.dot_general(g, v, NT, preferred_element_type=jnp.float32)
    grad_dot = jnp.sum(g.astype(jnp.float32) * out, axis=-1, keepdims=True)
    grad_score = (prob * (grad_prob - grad_dot)).astype(jnp.bfloat16)
    return prob_low, grad_score


def chain_kernel(x_ref, halo_ref, g0_ref, m_ref, *rest, first, count):
    if len(rest) == 3:
        prev_ref, o_ref, g_out_ref = rest
    else:
        prev_ref = None
        o_ref, g_out_ref = rest
    width = o_ref.shape[2]
    heads = width // DH
    halo_first = first + count - halo_ref.shape[0]
    allowed = m_ref[...] != 0
    if prev_ref is None:
        o_ref[o_ref.shape[0] - 1] = g0_ref[...]
    else:
        top = first + count - 1
        o_ref[top:] = prev_ref[top:]

    def step(i, g):
        layer = first + count - 1 - i
        local = layer - halo_first
        k = jnp.concatenate(
            [halo_ref[local, :, :DH], x_ref[layer, :, width:width + DH]], axis=0
        )
        v = jnp.concatenate(
            [halo_ref[local, :, DH:], x_ref[layer, :, width + DH:]], axis=0
        )
        outs = []
        for h in range(heads):
            cols = slice(h * DH, (h + 1) * DH)
            q = x_ref[layer, :, cols]
            gh = g[:, cols]
            _, grad_score = head_core(q, k, v, gh, allowed)
            dq = jnp.dot(grad_score, k, preferred_element_type=jnp.float32) * SCALE
            outs.append((gh.astype(jnp.float32) + dq).astype(jnp.bfloat16))
        g_new = jnp.concatenate(outs, axis=-1) if heads > 1 else outs[0]
        o_ref[layer - 1] = g_new
        return g_new

    g_out_ref[...] = lax.fori_loop(0, count, step, g0_ref[...], unroll=True)


def chain_call(sent, halo, grad_top, allowed_i32, first, count, prev=None, interpret=False):
    layers, rows, _ = sent.shape
    width = grad_top.shape[1]
    operands = [sent, halo, grad_top, allowed_i32]
    if prev is not None:
        operands.append(prev)
    return pl.pallas_call(
        functools.partial(chain_kernel, first=first, count=count),
        out_shape=(
            jax.ShapeDtypeStruct((layers, rows, width), jnp.bfloat16),
            jax.ShapeDtypeStruct((rows, width), jnp.bfloat16),
        ),
        interpret=interpret,
    )(*operands)


def pack_kernel(q_ref, k_ref, v_ref, send_ref, kv_ref, *, blocks_per_kv):
    blocks, _, total = send_ref.shape
    bw = total - 2 * DH
    q = q_ref[0, 0]
    k = k_ref[0, 0]
    v = v_ref[0, 0]
    for b in range(blocks):
        g = b // blocks_per_kv
        send_ref[b, :, :bw] = q[:, b * bw:(b + 1) * bw]
        send_ref[b, :, bw:bw + DH] = k[:, g * DH:(g + 1) * DH]
        send_ref[b, :, bw + DH:] = v[:, g * DH:(g + 1) * DH]
    kv_ref[0, 0, 0] = k
    kv_ref[1, 0, 0] = v


def pack_call(queries, keys, values, head_blocks, blocks_per_kv, interpret=False):
    _, micro_count, rows, width = queries.shape
    key_width = keys.shape[3]
    bw = width // head_blocks
    kv_in = pl.BlockSpec((1, 1, rows, key_width), lambda m: (0, m, 0, 0))
    return pl.pallas_call(
        functools.partial(pack_kernel, blocks_per_kv=blocks_per_kv),
        grid=(micro_count,),
        in_specs=[pl.BlockSpec((1, 1, rows, width), lambda m: (0, m, 0, 0)), kv_in, kv_in],
        out_specs=[pl.BlockSpec((head_blocks, rows, bw + 2 * DH), lambda m: (m, 0, 0)),
                   pl.BlockSpec((2, 1, 1, rows, key_width), lambda m: (0, 0, m, 0, 0))],
        out_shape=[
            jax.ShapeDtypeStruct((micro_count * head_blocks, rows, bw + 2 * DH), jnp.bfloat16),
            jax.ShapeDtypeStruct((2,) + keys.shape, jnp.bfloat16),
        ],
        interpret=interpret,
    )(queries, keys, values)


def layer_pre_kernel(q_ref, kvo_ref, kvh_ref, m_ref, p_ref, o_ref):
    heads = q_ref.shape[3] // DH
    allowed = m_ref[0] != 0
    k = jnp.concatenate([kvh_ref[0, 0, 0], kvo_ref[0, 0, 0]], axis=0)
    v = jnp.concatenate([kvh_ref[1, 0, 0], kvo_ref[1, 0, 0]], axis=0)
    for h in range(heads):
        q = q_ref[0, 0, :, h * DH:(h + 1) * DH]
        scores = lax.dot_general(q, k, NT, preferred_element_type=jnp.float32) * SCALE
        masked = jnp.where(allowed, scores, -jnp.inf)
        row_max = jnp.max(masked, axis=-1, keepdims=True)
        weights = jnp.exp(masked - row_max)
        prob = weights / jnp.sum(weights, axis=-1, keepdims=True)
        p_ref[0, h] = prob
        o_ref[0, h] = jnp.dot(prob.astype(jnp.bfloat16), v, preferred_element_type=jnp.float32)


def layer_pre_call(queries, kv_own, kv_halo, allowed_i32, interpret=False):
    _, micro_count, rows, width = queries.shape
    kv_heads = kv_own.shape[4] // DH
    group = width // (kv_heads * DH)
    kv_spec = pl.BlockSpec((2, 1, 1, rows, DH), lambda m, g: (0, 0, m, 0, g))
    return pl.pallas_call(
        layer_pre_kernel,
        grid=(micro_count, kv_heads),
        in_specs=[pl.BlockSpec((1, 1, rows, group * DH), lambda m, g: (0, m, 0, g)),
                  kv_spec, kv_spec,
                  pl.BlockSpec((1, rows, 2 * rows), lambda m, g: (m, 0, 0))],
        out_specs=[pl.BlockSpec((1, group, rows, 2 * rows), lambda m, g: (m, g, 0, 0)),
                   pl.BlockSpec((1, group, rows, DH), lambda m, g: (m, g, 0, 0))],
        out_shape=[
            jax.ShapeDtypeStruct((micro_count, kv_heads * group, rows, 2 * rows), jnp.float32),
            jax.ShapeDtypeStruct((micro_count, kv_heads * group, rows, DH), jnp.float32),
        ],
        interpret=interpret,
    )(queries, kv_own, kv_halo, allowed_i32)


def layer_kernel(q_ref, kvo_ref, kvh_ref, ga_ref, gb_ref, p_ref, o_ref, *rest):
    dk_ref, dv_ref, back_ref, gl_ref = rest[-4:]
    heads = q_ref.shape[3] // DH
    rows = q_ref.shape[2]
    k = jnp.concatenate([kvh_ref[0, 0, 0], kvo_ref[0, 0, 0]], axis=0)
    v = jnp.concatenate([kvh_ref[1, 0, 0], kvo_ref[1, 0, 0]], axis=0)
    grad = jnp.concatenate([ga_ref[0], gb_ref[0]], axis=-1)
    dk = None
    dv = None
    for h in range(heads):
        cols = slice(h * DH, (h + 1) * DH)
        q = q_ref[0, 0, :, cols]
        g = grad[:, cols]
        prob = p_ref[0, h]
        prob_low = prob.astype(jnp.bfloat16)
        grad_prob = lax.dot_general(g, v, NT, preferred_element_type=jnp.float32)
        grad_dot = jnp.sum(g.astype(jnp.float32) * o_ref[0, h], axis=-1, keepdims=True)
        grad_score = (prob * (grad_prob - grad_dot)).astype(jnp.bfloat16)
        dq = jnp.dot(grad_score, k, preferred_element_type=jnp.float32) * SCALE
        gl_ref[0, 0, :, cols] = (g.astype(jnp.float32) + dq).astype(jnp.bfloat16)
        dk_h = lax.dot_general(grad_score, q, TN, preferred_element_type=jnp.float32)
        dv_h = lax.dot_general(prob_low, g, TN, preferred_element_type=jnp.float32)
        dk = dk_h if dk is None else dk + dk_h
        dv = dv_h if dv is None else dv + dv_h
    dk = dk * SCALE
    back_ref[0, 0] = dk[:rows].astype(back_ref.dtype)
    back_ref[1, 0] = dv[:rows].astype(back_ref.dtype)
    dk_ref[0] = dk[rows:]
    dv_ref[0] = dv[rows:]


def layer_call(queries, kv_own, kv_halo, grad_t, prob, out, grad_prev, micro,
               blocks_per_kv, interpret=False):
    _, _, rows, width = queries.shape
    kv_heads = kv_own.shape[4] // DH
    group = width // (kv_heads * DH)
    gw = group * DH
    bw = grad_t.shape[2]
    kv_spec = pl.BlockSpec((2, 1, 1, rows, DH), lambda i, g: (0, 0, micro, 0, g))
    q_spec = pl.BlockSpec((1, 1, rows, gw), lambda i, g: (0, micro, 0, g))
    head_blocks = width // bw
    ga_spec = pl.BlockSpec(
        (1, rows, bw), lambda i, g: (micro * head_blocks + g * blocks_per_kv, 0, 0))
    gb_spec = pl.BlockSpec(
        (1, rows, bw), lambda i, g: (micro * head_blocks + g * blocks_per_kv + 1, 0, 0))
    p_spec = pl.BlockSpec((1, group, rows, 2 * rows), lambda i, g: (micro, g, 0, 0))
    o_spec = pl.BlockSpec((1, group, rows, DH), lambda i, g: (micro, g, 0, 0))
    own_out = pl.BlockSpec((1, rows, DH), lambda i, g: (0, 0, g))
    own_shape = jax.ShapeDtypeStruct((1, rows, kv_heads * DH), jnp.float32)
    in_specs = [q_spec, kv_spec, kv_spec, ga_spec, gb_spec, p_spec, o_spec]
    operands = [queries, kv_own, kv_halo, grad_t, grad_t, prob, out]
    aliases = {}
    if grad_prev is not None:
        in_specs.append(pl.BlockSpec(memory_space=pl.ANY))
        operands.append(grad_prev)
        aliases = {len(operands) - 1: 3}
    return pl.pallas_call(
        layer_kernel,
        grid=(1, kv_heads),
        in_specs=in_specs,
        out_specs=[own_out, own_out,
                   pl.BlockSpec((2, 1, rows, DH), lambda i, g: (0, 0, 0, g)),
                   q_spec],
        out_shape=[own_shape, own_shape,
                   jax.ShapeDtypeStruct((2, 1, rows, kv_heads * DH), jnp.bfloat16),
                   jax.ShapeDtypeStruct(queries.shape, jnp.bfloat16)],
        input_output_aliases=aliases,
        interpret=interpret,
    )(*operands)


def device_body(queries, keys, values, out_grad, segments):
    micro_count = queries.shape[1]
    row_count = queries.shape[2]
    query_width = queries.shape[3]
    key_width = keys.shape[3]
    section_count = lax.axis_size("pipe")
    section_index = lax.axis_index("pipe")
    seq_index = lax.axis_index("seq")
    kv_heads = key_width // DH
    q_heads = query_width // DH
    group_size = q_heads // kv_heads
    head_blocks = section_count // micro_count
    block_heads = q_heads // head_blocks
    block_width = block_heads * DH
    blocks_per_kv = group_size // block_heads
    send, kv_own = pack_call(queries, keys, values, head_blocks, blocks_per_kv)
    seg_padded = jnp.concatenate(
        [jnp.full((micro_count, row_count), -1, jnp.int32), segments], axis=1
    )
    query_pos = seq_index * row_count + jnp.arange(row_count, dtype=jnp.int32)
    key_pos = seq_index * row_count - row_count + jnp.arange(2 * row_count, dtype=jnp.int32)
    seg_query = lax.dynamic_slice_in_dim(
        seg_padded, seq_index * row_count + row_count, row_count, axis=1
    )
    seg_key = lax.dynamic_slice_in_dim(seg_padded, seq_index * row_count, 2 * row_count, axis=1)
    near = (
        (key_pos[None, :] <= query_pos[:, None])
        & (query_pos[:, None] - key_pos[None, :] < WINDOW)
        & (key_pos[None, :] >= 0)
    )
    masks = (near[None] & (seg_query[:, :, None] == seg_key[:, None, :])).astype(jnp.int32)
    kv_halo = from_behind(kv_own, "seq", 1)

    my_block = section_index % head_blocks
    my_micro = section_index // head_blocks
    sent = lax.all_to_all(send, "pipe", 0, 0)
    prob, out = layer_pre_call(queries, kv_own, kv_halo, masks)
    split_at = section_count // 2
    halo_hi = from_behind(sent[split_at:, :, block_width:], "seq", 1)
    halo_lo = from_behind(sent[1:split_at, :, block_width:], "seq", 1)
    grad_top = lax.dynamic_slice(
        out_grad, (my_micro, 0, my_block * block_width), (1, row_count, block_width)
    )[0]
    allowed = lax.dynamic_index_in_dim(masks, my_micro, 0, keepdims=False)
    above_hi, grad_mid = chain_call(
        sent, halo_hi, grad_top, allowed, split_at, section_count - split_at)
    grads_above, _ = chain_call(sent, halo_lo, grad_mid, allowed, 1, split_at - 1, above_hi)
    grad_t = lax.all_to_all(grads_above, "pipe", 0, 0)

    query_all = None
    key_parts = []
    value_parts = []
    for micro in range(micro_count):
        key_own_grad, value_own_grad, kv_back, query_all = layer_call(
            queries, kv_own, kv_halo, grad_t, prob, out, query_all, micro, blocks_per_kv
        )
        kv_next = from_behind(kv_back, "seq", -1)
        key_parts.append(key_own_grad + kv_next[0].astype(jnp.float32))
        value_parts.append(value_own_grad + kv_next[1].astype(jnp.float32))
    query_all = query_all[0]
    key_grads = jnp.concatenate(key_parts, axis=0).astype(jnp.bfloat16)
    value_grads = jnp.concatenate(value_parts, axis=0).astype(jnp.bfloat16)
    return (query_all[None], key_grads[None], value_grads[None])


def solution(mesh):
    placed = (
        P("pipe", None, "seq", None),
        P("pipe", None, "seq", None),
        P("pipe", None, "seq", None),
        P(None, "seq", None),
        P(),
    )
    return jax.shard_map(
        device_body,
        mesh=mesh,
        in_specs=placed,
        out_specs=(
            P("pipe", None, "seq", None),
            P("pipe", None, "seq", None),
            P("pipe", None, "seq", None),
        ),
        check_vma=False,
    )
```

```python
import functools

import jax
import jax.numpy as jnp
from jax import lax
from jax.experimental import pallas as pl
from jax.sharding import PartitionSpec as P


DH = 128
WINDOW = 128
SCALE = DH ** (-0.5)
NT = (((1,), (1,)), ((), ()))
TN = (((0,), (0,)), ((), ()))


def from_behind(block, axis, distance):
    devices = range(lax.axis_size(axis))
    route = [(i - distance, i) for i in devices if i - distance in devices]
    return lax.ppermute(block, axis, route)


def head_core(q, k, v, g, allowed):
    scores = lax.dot_general(q, k, NT, preferred_element_type=jnp.float32) * SCALE
    masked = jnp.where(allowed, scores, -jnp.inf)
    row_max = jnp.max(masked, axis=-1, keepdims=True)
    weights = jnp.exp(masked - row_max)
    prob = weights / jnp.sum(weights, axis=-1, keepdims=True)
    prob_low = prob.astype(jnp.bfloat16)
    out = jnp.dot(prob_low, v, preferred_element_type=jnp.float32)
    grad_prob = lax.dot_general(g, v, NT, preferred_element_type=jnp.float32)
    grad_dot = jnp.sum(g.astype(jnp.float32) * out, axis=-1, keepdims=True)
    grad_score = (prob * (grad_prob - grad_dot)).astype(jnp.bfloat16)
    return prob_low, grad_score


def chain_kernel(x_ref, g0_ref, m_ref, *rest, first, count):
    if len(rest) == 3:
        prev_ref, o_ref, g_out_ref = rest
    else:
        prev_ref = None
        o_ref, g_out_ref = rest
    width = o_ref.shape[2]
    heads = width // DH
    allowed = m_ref[...] != 0
    if prev_ref is None:
        o_ref[o_ref.shape[0] - 1] = g0_ref[...]
    else:
        top = first + count - 1
        o_ref[top:] = prev_ref[top:]

    def step(i, g):
        layer = first + count - 1 - i
        k = jnp.concatenate(
            [x_ref[layer, :, width + 2 * DH:width + 3 * DH], x_ref[layer, :, width:width + DH]],
            axis=0,
        )
        v = jnp.concatenate(
            [x_ref[layer, :, width + 3 * DH:], x_ref[layer, :, width + DH:width + 2 * DH]],
            axis=0,
        )
        outs = []
        for h in range(heads):
            cols = slice(h * DH, (h + 1) * DH)
            q = x_ref[layer, :, cols]
            gh = g[:, cols]
            _, grad_score = head_core(q, k, v, gh, allowed)
            dq = jnp.dot(grad_score, k, preferred_element_type=jnp.float32) * SCALE
            outs.append((gh.astype(jnp.float32) + dq).astype(jnp.bfloat16))
        g_new = jnp.concatenate(outs, axis=-1) if heads > 1 else outs[0]
        o_ref[layer - 1] = g_new
        return g_new

    g_out_ref[...] = lax.fori_loop(0, count, step, g0_ref[...], unroll=True)


def chain_call(sent, grad_top, allowed_i32, first, count, prev=None, interpret=False):
    layers, rows, _ = sent.shape
    width = grad_top.shape[1]
    operands = [sent, grad_top, allowed_i32]
    if prev is not None:
        operands.append(prev)
    return pl.pallas_call(
        functools.partial(chain_kernel, first=first, count=count),
        out_shape=(
            jax.ShapeDtypeStruct((layers, rows, width), jnp.bfloat16),
            jax.ShapeDtypeStruct((rows, width), jnp.bfloat16),
        ),
        interpret=interpret,
    )(*operands)


def pack_kernel(q_ref, kv_ref, kvh_ref, send_ref, *, blocks_per_kv):
    blocks, _, total = send_ref.shape
    bw = total - 4 * DH
    q = q_ref[0, 0]
    parts = (kv_ref[0, 0, 0], kv_ref[1, 0, 0], kvh_ref[0, 0, 0], kvh_ref[1, 0, 0])
    for b in range(blocks):
        g = b // blocks_per_kv
        send_ref[b, :, :bw] = q[:, b * bw:(b + 1) * bw]
        for j, part in enumerate(parts):
            send_ref[b, :, bw + j * DH:bw + (j + 1) * DH] = part[:, g * DH:(g + 1) * DH]


def pack_call(queries, kv_own, kv_halo, head_blocks, blocks_per_kv, interpret=False):
    _, micro_count, rows, width = queries.shape
    key_width = kv_own.shape[4]
    bw = width // head_blocks
    kv_in = pl.BlockSpec((2, 1, 1, rows, key_width), lambda m: (0, 0, m, 0, 0))
    return pl.pallas_call(
        functools.partial(pack_kernel, blocks_per_kv=blocks_per_kv),
        grid=(micro_count,),
        in_specs=[pl.BlockSpec((1, 1, rows, width), lambda m: (0, m, 0, 0)), kv_in, kv_in],
        out_specs=pl.BlockSpec((head_blocks, rows, bw + 4 * DH), lambda m: (m, 0, 0)),
        out_shape=jax.ShapeDtypeStruct(
            (micro_count * head_blocks, rows, bw + 4 * DH), jnp.bfloat16),
        interpret=interpret,
    )(queries, kv_own, kv_halo)


def layer_pre_kernel(q_ref, kvo_ref, kvh_ref, m_ref, p_ref, o_ref):
    heads = q_ref.shape[3] // DH
    allowed = m_ref[0] != 0
    k = jnp.concatenate([kvh_ref[0, 0, 0], kvo_ref[0, 0, 0]], axis=0)
    v = jnp.concatenate([kvh_ref[1, 0, 0], kvo_ref[1, 0, 0]], axis=0)
    for h in range(heads):
        q = q_ref[0, 0, :, h * DH:(h + 1) * DH]
        scores = lax.dot_general(q, k, NT, preferred_element_type=jnp.float32) * SCALE
        masked = jnp.where(allowed, scores, -jnp.inf)
        row_max = jnp.max(masked, axis=-1, keepdims=True)
        weights = jnp.exp(masked - row_max)
        prob = weights / jnp.sum(weights, axis=-1, keepdims=True)
        p_ref[0, h] = prob
        o_ref[0, h] = jnp.dot(prob.astype(jnp.bfloat16), v, preferred_element_type=jnp.float32)


def layer_pre_call(queries, kv_own, kv_halo, allowed_i32, interpret=False):
    _, micro_count, rows, width = queries.shape
    kv_heads = kv_own.shape[4] // DH
    group = width // (kv_heads * DH)
    kv_spec = pl.BlockSpec((2, 1, 1, rows, DH), lambda m, g: (0, 0, m, 0, g))
    return pl.pallas_call(
        layer_pre_kernel,
        grid=(micro_count, kv_heads),
        in_specs=[pl.BlockSpec((1, 1, rows, group * DH), lambda m, g: (0, m, 0, g)),
                  kv_spec, kv_spec,
                  pl.BlockSpec((1, rows, 2 * rows), lambda m, g: (m, 0, 0))],
        out_specs=[pl.BlockSpec((1, group, rows, 2 * rows), lambda m, g: (m, g, 0, 0)),
                   pl.BlockSpec((1, group, rows, DH), lambda m, g: (m, g, 0, 0))],
        out_shape=[
            jax.ShapeDtypeStruct((micro_count, kv_heads * group, rows, 2 * rows), jnp.float32),
            jax.ShapeDtypeStruct((micro_count, kv_heads * group, rows, DH), jnp.float32),
        ],
        interpret=interpret,
    )(queries, kv_own, kv_halo, allowed_i32)


def layer_kernel(q_ref, kvo_ref, kvh_ref, ga_ref, gb_ref, p_ref, o_ref, *rest):
    dk_ref, dv_ref, back_ref, gl_ref = rest[-4:]
    heads = q_ref.shape[3] // DH
    rows = q_ref.shape[2]
    k = jnp.concatenate([kvh_ref[0, 0, 0], kvo_ref[0, 0, 0]], axis=0)
    v = jnp.concatenate([kvh_ref[1, 0, 0], kvo_ref[1, 0, 0]], axis=0)
    grad = jnp.concatenate([ga_ref[0], gb_ref[0]], axis=-1)
    dk = None
    dv = None
    for h in range(heads):
        cols = slice(h * DH, (h + 1) * DH)
        q = q_ref[0, 0, :, cols]
        g = grad[:, cols]
        prob = p_ref[0, h]
        prob_low = prob.astype(jnp.bfloat16)
        grad_prob = lax.dot_general(g, v, NT, preferred_element_type=jnp.float32)
        grad_dot = jnp.sum(g.astype(jnp.float32) * o_ref[0, h], axis=-1, keepdims=True)
        grad_score = (prob * (grad_prob - grad_dot)).astype(jnp.bfloat16)
        dq = jnp.dot(grad_score, k, preferred_element_type=jnp.float32) * SCALE
        gl_ref[0, 0, :, cols] = (g.astype(jnp.float32) + dq).astype(jnp.bfloat16)
        dk_h = lax.dot_general(grad_score, q, TN, preferred_element_type=jnp.float32)
        dv_h = lax.dot_general(prob_low, g, TN, preferred_element_type=jnp.float32)
        dk = dk_h if dk is None else dk + dk_h
        dv = dv_h if dv is None else dv + dv_h
    dk = dk * SCALE
    back_ref[0, 0] = dk[:rows].astype(back_ref.dtype)
    back_ref[1, 0] = dv[:rows].astype(back_ref.dtype)
    dk_ref[0] = dk[rows:]
    dv_ref[0] = dv[rows:]


def layer_call(queries, kv_own, kv_halo, grad_t, prob, out, grad_prev, micro,
               blocks_per_kv, interpret=False):
    _, _, rows, width = queries.shape
    kv_heads = kv_own.shape[4] // DH
    group = width // (kv_heads * DH)
    gw = group * DH
    bw = grad_t.shape[2]
    kv_spec = pl.BlockSpec((2, 1, 1, rows, DH), lambda i, g: (0, 0, micro, 0, g))
    q_spec = pl.BlockSpec((1, 1, rows, gw), lambda i, g: (0, micro, 0, g))
    head_blocks = width // bw
    ga_spec = pl.BlockSpec(
        (1, rows, bw), lambda i, g: (micro * head_blocks + g * blocks_per_kv, 0, 0))
    gb_spec = pl.BlockSpec(
        (1, rows, bw), lambda i, g: (micro * head_blocks + g * blocks_per_kv + 1, 0, 0))
    p_spec = pl.BlockSpec((1, group, rows, 2 * rows), lambda i, g: (micro, g, 0, 0))
    o_spec = pl.BlockSpec((1, group, rows, DH), lambda i, g: (micro, g, 0, 0))
    own_out = pl.BlockSpec((1, rows, DH), lambda i, g: (0, 0, g))
    own_shape = jax.ShapeDtypeStruct((1, rows, kv_heads * DH), jnp.float32)
    in_specs = [q_spec, kv_spec, kv_spec, ga_spec, gb_spec, p_spec, o_spec]
    operands = [queries, kv_own, kv_halo, grad_t, grad_t, prob, out]
    aliases = {}
    if grad_prev is not None:
        in_specs.append(pl.BlockSpec(memory_space=pl.ANY))
        operands.append(grad_prev)
        aliases = {len(operands) - 1: 3}
    return pl.pallas_call(
        layer_kernel,
        grid=(1, kv_heads),
        in_specs=in_specs,
        out_specs=[own_out, own_out,
                   pl.BlockSpec((2, 1, rows, DH), lambda i, g: (0, 0, 0, g)),
                   q_spec],
        out_shape=[own_shape, own_shape,
                   jax.ShapeDtypeStruct((2, 1, rows, kv_heads * DH), jnp.bfloat16),
                   jax.ShapeDtypeStruct(queries.shape, jnp.bfloat16)],
        input_output_aliases=aliases,
        interpret=interpret,
    )(*operands)


def device_body(queries, keys, values, out_grad, segments):
    micro_count = queries.shape[1]
    row_count = queries.shape[2]
    query_width = queries.shape[3]
    key_width = keys.shape[3]
    section_count = lax.axis_size("pipe")
    section_index = lax.axis_index("pipe")
    seq_index = lax.axis_index("seq")
    kv_heads = key_width // DH
    q_heads = query_width // DH
    group_size = q_heads // kv_heads
    head_blocks = section_count // micro_count
    block_heads = q_heads // head_blocks
    block_width = block_heads * DH
    blocks_per_kv = group_size // block_heads
    kv_own = jnp.stack([keys, values])
    seg_padded = jnp.concatenate(
        [jnp.full((micro_count, row_count), -1, jnp.int32), segments], axis=1
    )
    query_pos = seq_index * row_count + jnp.arange(row_count, dtype=jnp.int32)
    key_pos = seq_index * row_count - row_count + jnp.arange(2 * row_count, dtype=jnp.int32)
    seg_query = lax.dynamic_slice_in_dim(
        seg_padded, seq_index * row_count + row_count, row_count, axis=1
    )
    seg_key = lax.dynamic_slice_in_dim(seg_padded, seq_index * row_count, 2 * row_count, axis=1)
    near = (
        (key_pos[None, :] <= query_pos[:, None])
        & (query_pos[:, None] - key_pos[None, :] < WINDOW)
        & (key_pos[None, :] >= 0)
    )
    masks = (near[None] & (seg_query[:, :, None] == seg_key[:, None, :])).astype(jnp.int32)
    kv_halo = from_behind(kv_own, "seq", 1)

    my_block = section_index % head_blocks
    my_micro = section_index // head_blocks
    send = pack_call(queries, kv_own, kv_halo, head_blocks, blocks_per_kv)
    sent = lax.all_to_all(send, "pipe", 0, 0)
    prob, out = layer_pre_call(queries, kv_own, kv_halo, masks)
    grad_top = lax.dynamic_slice(
        out_grad, (my_micro, 0, my_block * block_width), (1, row_count, block_width)
    )[0]
    allowed = lax.dynamic_index_in_dim(masks, my_micro, 0, keepdims=False)
    grads_above, _ = chain_call(sent, grad_top, allowed, 1, section_count - 1)
    grad_t = lax.all_to_all(grads_above, "pipe", 0, 0)

    query_all = None
    key_parts = []
    value_parts = []
    for micro in range(micro_count):
        key_own_grad, value_own_grad, kv_back, query_all = layer_call(
            queries, kv_own, kv_halo, grad_t, prob, out, query_all, micro, blocks_per_kv
        )
        kv_next = from_behind(kv_back, "seq", -1)
        key_parts.append(key_own_grad + kv_next[0].astype(jnp.float32))
        value_parts.append(value_own_grad + kv_next[1].astype(jnp.float32))
    query_all = query_all[0]
    key_grads = jnp.concatenate(key_parts, axis=0).astype(jnp.bfloat16)
    value_grads = jnp.concatenate(value_parts, axis=0).astype(jnp.bfloat16)
    return (query_all[None], key_grads[None], value_grads[None])


def solution(mesh):
    placed = (
        P("pipe", None, "seq", None),
        P("pipe", None, "seq", None),
        P("pipe", None, "seq", None),
        P(None, "seq", None),
        P(),
    )
    return jax.shard_map(
        device_body,
        mesh=mesh,
        in_specs=placed,
        out_specs=(
            P("pipe", None, "seq", None),
            P("pipe", None, "seq", None),
            P("pipe", None, "seq", None),
        ),
        check_vma=False,
    )
```

```python
import functools

import jax
import jax.numpy as jnp
from jax import lax
from jax.experimental import pallas as pl
from jax.experimental.pallas import tpu as pltpu
from jax.sharding import PartitionSpec as P


DH = 128
WINDOW = 128
SCALE = DH ** (-0.5)
NT = (((1,), (1,)), ((), ()))
TN = (((0,), (0,)), ((), ()))


def from_behind(block, axis, distance):
    devices = range(lax.axis_size(axis))
    route = [(i - distance, i) for i in devices if i - distance in devices]
    return lax.ppermute(block, axis, route)


def head_core(q, k, v, g, allowed):
    scores = lax.dot_general(q, k, NT, preferred_element_type=jnp.float32) * SCALE
    masked = jnp.where(allowed, scores, -jnp.inf)
    row_max = jnp.max(masked, axis=-1, keepdims=True)
    weights = jnp.exp(masked - row_max)
    prob = weights / jnp.sum(weights, axis=-1, keepdims=True)
    prob_low = prob.astype(jnp.bfloat16)
    out = jnp.dot(prob_low, v, preferred_element_type=jnp.float32)
    grad_prob = lax.dot_general(g, v, NT, preferred_element_type=jnp.float32)
    grad_dot = jnp.sum(g.astype(jnp.float32) * out, axis=-1, keepdims=True)
    grad_score = (prob * (grad_prob - grad_dot)).astype(jnp.bfloat16)
    return prob_low, grad_score


def chain_kernel(x_hbm, halo_hbm, g0_ref, m_ref, *rest, first, count):
    if len(rest) == 6:
        prev_hbm, o_ref, g_out_ref, x_buf, h_buf, sems = rest
    else:
        prev_hbm = None
        o_ref, g_out_ref, x_buf, h_buf, sems = rest
    width = o_ref.shape[2]
    heads = width // DH
    halo_first = first + count - halo_hbm.shape[0]
    allowed = m_ref[...] != 0
    top = first + count - 1
    copies = []
    for i in range(count):
        layer = top - i
        cx = pltpu.make_async_copy(x_hbm.at[layer], x_buf.at[i], sems.at[0, i])
        ch = pltpu.make_async_copy(halo_hbm.at[layer - halo_first], h_buf.at[i], sems.at[1, i])
        cx.start()
        ch.start()
        copies.append((cx, ch))
    if prev_hbm is None:
        o_ref[o_ref.shape[0] - 1] = g0_ref[...]
        keep = None
    else:
        keep = pltpu.make_async_copy(prev_hbm.at[top:], o_ref.at[top:], sems.at[2, 0])
        keep.start()
    g = g0_ref[...]
    for i in range(count):
        layer = top - i
        cx, ch = copies[i]
        cx.wait()
        ch.wait()
        k = jnp.concatenate([h_buf[i, :, :DH], x_buf[i, :, width:width + DH]], axis=0)
        v = jnp.concatenate([h_buf[i, :, DH:], x_buf[i, :, width + DH:]], axis=0)
        outs = []
        for h in range(heads):
            cols = slice(h * DH, (h + 1) * DH)
            q = x_buf[i, :, cols]
            gh = g[:, cols]
            _, grad_score = head_core(q, k, v, gh, allowed)
            dq = jnp.dot(grad_score, k, preferred_element_type=jnp.float32) * SCALE
            outs.append((gh.astype(jnp.float32) + dq).astype(jnp.bfloat16))
        g = jnp.concatenate(outs, axis=-1) if heads > 1 else outs[0]
        o_ref[layer - 1] = g
    g_out_ref[...] = g
    if keep is not None:
        keep.wait()


def chain_call(sent, halo, grad_top, allowed_i32, first, count, prev=None, interpret=False):
    layers, rows, total = sent.shape
    width = grad_top.shape[1]
    operands = [sent, halo, grad_top, allowed_i32]
    any_spec = pl.BlockSpec(memory_space=pl.ANY)
    vmem_spec = pl.BlockSpec(memory_space=pltpu.VMEM)
    in_specs = [any_spec, any_spec, vmem_spec, vmem_spec]
    if prev is not None:
        operands.append(prev)
        in_specs.append(any_spec)
    return pl.pallas_call(
        functools.partial(chain_kernel, first=first, count=count),
        in_specs=in_specs,
        out_specs=(vmem_spec, vmem_spec),
        out_shape=(
            jax.ShapeDtypeStruct((layers, rows, width), jnp.bfloat16),
            jax.ShapeDtypeStruct((rows, width), jnp.bfloat16),
        ),
        scratch_shapes=[
            pltpu.VMEM((count, rows, total), sent.dtype),
            pltpu.VMEM((count, rows, halo.shape[2]), halo.dtype),
            pltpu.SemaphoreType.DMA((3, count)),
        ],
        interpret=interpret,
    )(*operands)


def pack_kernel(q_ref, k_ref, v_ref, send_ref, kv_ref, *, blocks_per_kv):
    blocks, _, total = send_ref.shape
    bw = total - 2 * DH
    q = q_ref[0, 0]
    k = k_ref[0, 0]
    v = v_ref[0, 0]
    for b in range(blocks):
        g = b // blocks_per_kv
        send_ref[b, :, :bw] = q[:, b * bw:(b + 1) * bw]
        send_ref[b, :, bw:bw + DH] = k[:, g * DH:(g + 1) * DH]
        send_ref[b, :, bw + DH:] = v[:, g * DH:(g + 1) * DH]
    kv_ref[0, 0, 0] = k
    kv_ref[1, 0, 0] = v


def pack_call(queries, keys, values, head_blocks, blocks_per_kv, interpret=False):
    _, micro_count, rows, width = queries.shape
    key_width = keys.shape[3]
    bw = width // head_blocks
    kv_in = pl.BlockSpec((1, 1, rows, key_width), lambda m: (0, m, 0, 0))
    return pl.pallas_call(
        functools.partial(pack_kernel, blocks_per_kv=blocks_per_kv),
        grid=(micro_count,),
        in_specs=[pl.BlockSpec((1, 1, rows, width), lambda m: (0, m, 0, 0)), kv_in, kv_in],
        out_specs=[pl.BlockSpec((head_blocks, rows, bw + 2 * DH), lambda m: (m, 0, 0)),
                   pl.BlockSpec((2, 1, 1, rows, key_width), lambda m: (0, 0, m, 0, 0))],
        out_shape=[
            jax.ShapeDtypeStruct((micro_count * head_blocks, rows, bw + 2 * DH), jnp.bfloat16),
            jax.ShapeDtypeStruct((2,) + keys.shape, jnp.bfloat16),
        ],
        interpret=interpret,
    )(queries, keys, values)


def layer_pre_kernel(q_ref, kvo_ref, kvh_ref, m_ref, p_ref, o_ref):
    heads = q_ref.shape[3] // DH
    allowed = m_ref[0] != 0
    k = jnp.concatenate([kvh_ref[0, 0, 0], kvo_ref[0, 0, 0]], axis=0)
    v = jnp.concatenate([kvh_ref[1, 0, 0], kvo_ref[1, 0, 0]], axis=0)
    for h in range(heads):
        q = q_ref[0, 0, :, h * DH:(h + 1) * DH]
        scores = lax.dot_general(q, k, NT, preferred_element_type=jnp.float32) * SCALE
        masked = jnp.where(allowed, scores, -jnp.inf)
        row_max = jnp.max(masked, axis=-1, keepdims=True)
        weights = jnp.exp(masked - row_max)
        prob = weights / jnp.sum(weights, axis=-1, keepdims=True)
        p_ref[0, h] = prob
        o_ref[0, h] = jnp.dot(prob.astype(jnp.bfloat16), v, preferred_element_type=jnp.float32)


def layer_pre_call(queries, kv_own, kv_halo, allowed_i32, interpret=False):
    _, micro_count, rows, width = queries.shape
    kv_heads = kv_own.shape[4] // DH
    group = width // (kv_heads * DH)
    kv_spec = pl.BlockSpec((2, 1, 1, rows, DH), lambda m, g: (0, 0, m, 0, g))
    return pl.pallas_call(
        layer_pre_kernel,
        grid=(micro_count, kv_heads),
        in_specs=[pl.BlockSpec((1, 1, rows, group * DH), lambda m, g: (0, m, 0, g)),
                  kv_spec, kv_spec,
                  pl.BlockSpec((1, rows, 2 * rows), lambda m, g: (m, 0, 0))],
        out_specs=[pl.BlockSpec((1, group, rows, 2 * rows), lambda m, g: (m, g, 0, 0)),
                   pl.BlockSpec((1, group, rows, DH), lambda m, g: (m, g, 0, 0))],
        out_shape=[
            jax.ShapeDtypeStruct((micro_count, kv_heads * group, rows, 2 * rows), jnp.float32),
            jax.ShapeDtypeStruct((micro_count, kv_heads * group, rows, DH), jnp.float32),
        ],
        interpret=interpret,
    )(queries, kv_own, kv_halo, allowed_i32)


def layer_kernel(q_ref, kvo_ref, kvh_ref, ga_ref, gb_ref, p_ref, o_ref, *rest):
    dk_ref, dv_ref, back_ref, gl_ref = rest[-4:]
    heads = q_ref.shape[3] // DH
    rows = q_ref.shape[2]
    k = jnp.concatenate([kvh_ref[0, 0, 0], kvo_ref[0, 0, 0]], axis=0)
    v = jnp.concatenate([kvh_ref[1, 0, 0], kvo_ref[1, 0, 0]], axis=0)
    grad = jnp.concatenate([ga_ref[0], gb_ref[0]], axis=-1)
    dk = None
    dv = None
    for h in range(heads):
        cols = slice(h * DH, (h + 1) * DH)
        q = q_ref[0, 0, :, cols]
        g = grad[:, cols]
        prob = p_ref[0, h]
        prob_low = prob.astype(jnp.bfloat16)
        grad_prob = lax.dot_general(g, v, NT, preferred_element_type=jnp.float32)
        grad_dot = jnp.sum(g.astype(jnp.float32) * o_ref[0, h], axis=-1, keepdims=True)
        grad_score = (prob * (grad_prob - grad_dot)).astype(jnp.bfloat16)
        dq = jnp.dot(grad_score, k, preferred_element_type=jnp.float32) * SCALE
        gl_ref[0, 0, :, cols] = (g.astype(jnp.float32) + dq).astype(jnp.bfloat16)
        dk_h = lax.dot_general(grad_score, q, TN, preferred_element_type=jnp.float32)
        dv_h = lax.dot_general(prob_low, g, TN, preferred_element_type=jnp.float32)
        dk = dk_h if dk is None else dk + dk_h
        dv = dv_h if dv is None else dv + dv_h
    dk = dk * SCALE
    back_ref[0, 0] = dk[:rows].astype(back_ref.dtype)
    back_ref[1, 0] = dv[:rows].astype(back_ref.dtype)
    dk_ref[0] = dk[rows:]
    dv_ref[0] = dv[rows:]


def layer_call(queries, kv_own, kv_halo, grad_t, prob, out, grad_prev, micro,
               blocks_per_kv, interpret=False):
    _, _, rows, width = queries.shape
    kv_heads = kv_own.shape[4] // DH
    group = width // (kv_heads * DH)
    gw = group * DH
    bw = grad_t.shape[2]
    kv_spec = pl.BlockSpec((2, 1, 1, rows, DH), lambda i, g: (0, 0, micro, 0, g))
    q_spec = pl.BlockSpec((1, 1, rows, gw), lambda i, g: (0, micro, 0, g))
    head_blocks = width // bw
    ga_spec = pl.BlockSpec(
        (1, rows, bw), lambda i, g: (micro * head_blocks + g * blocks_per_kv, 0, 0))
    gb_spec = pl.BlockSpec(
        (1, rows, bw), lambda i, g: (micro * head_blocks + g * blocks_per_kv + 1, 0, 0))
    p_spec = pl.BlockSpec((1, group, rows, 2 * rows), lambda i, g: (micro, g, 0, 0))
    o_spec = pl.BlockSpec((1, group, rows, DH), lambda i, g: (micro, g, 0, 0))
    own_out = pl.BlockSpec((1, rows, DH), lambda i, g: (0, 0, g))
    own_shape = jax.ShapeDtypeStruct((1, rows, kv_heads * DH), jnp.float32)
    in_specs = [q_spec, kv_spec, kv_spec, ga_spec, gb_spec, p_spec, o_spec]
    operands = [queries, kv_own, kv_halo, grad_t, grad_t, prob, out]
    aliases = {}
    if grad_prev is not None:
        in_specs.append(pl.BlockSpec(memory_space=pl.ANY))
        operands.append(grad_prev)
        aliases = {len(operands) - 1: 3}
    return pl.pallas_call(
        layer_kernel,
        grid=(1, kv_heads),
        in_specs=in_specs,
        out_specs=[own_out, own_out,
                   pl.BlockSpec((2, 1, rows, DH), lambda i, g: (0, 0, 0, g)),
                   q_spec],
        out_shape=[own_shape, own_shape,
                   jax.ShapeDtypeStruct((2, 1, rows, kv_heads * DH), jnp.bfloat16),
                   jax.ShapeDtypeStruct(queries.shape, jnp.bfloat16)],
        input_output_aliases=aliases,
        interpret=interpret,
    )(*operands)


def device_body(queries, keys, values, out_grad, segments):
    micro_count = queries.shape[1]
    row_count = queries.shape[2]
    query_width = queries.shape[3]
    key_width = keys.shape[3]
    section_count = lax.axis_size("pipe")
    section_index = lax.axis_index("pipe")
    seq_index = lax.axis_index("seq")
    kv_heads = key_width // DH
    q_heads = query_width // DH
    group_size = q_heads // kv_heads
    head_blocks = section_count // micro_count
    block_heads = q_heads // head_blocks
    block_width = block_heads * DH
    blocks_per_kv = group_size // block_heads
    send, kv_own = pack_call(queries, keys, values, head_blocks, blocks_per_kv)
    seg_padded = jnp.concatenate(
        [jnp.full((micro_count, row_count), -1, jnp.int32), segments], axis=1
    )
    query_pos = seq_index * row_count + jnp.arange(row_count, dtype=jnp.int32)
    key_pos = seq_index * row_count - row_count + jnp.arange(2 * row_count, dtype=jnp.int32)
    seg_query = lax.dynamic_slice_in_dim(
        seg_padded, seq_index * row_count + row_count, row_count, axis=1
    )
    seg_key = lax.dynamic_slice_in_dim(seg_padded, seq_index * row_count, 2 * row_count, axis=1)
    near = (
        (key_pos[None, :] <= query_pos[:, None])
        & (query_pos[:, None] - key_pos[None, :] < WINDOW)
        & (key_pos[None, :] >= 0)
    )
    masks = (near[None] & (seg_query[:, :, None] == seg_key[:, None, :])).astype(jnp.int32)
    kv_halo = from_behind(kv_own, "seq", 1)

    my_block = section_index % head_blocks
    my_micro = section_index // head_blocks
    sent = lax.all_to_all(send, "pipe", 0, 0)
    prob, out = layer_pre_call(queries, kv_own, kv_halo, masks)
    split_at = section_count // 2
    halo_hi = from_behind(sent[split_at:, :, block_width:], "seq", 1)
    halo_lo = from_behind(sent[1:split_at, :, block_width:], "seq", 1)
    grad_top = lax.dynamic_slice(
        out_grad, (my_micro, 0, my_block * block_width), (1, row_count, block_width)
    )[0]
    allowed = lax.dynamic_index_in_dim(masks, my_micro, 0, keepdims=False)
    above_hi, grad_mid = chain_call(
        sent, halo_hi, grad_top, allowed, split_at, section_count - split_at)
    grads_above, _ = chain_call(sent, halo_lo, grad_mid, allowed, 1, split_at - 1, above_hi)
    grad_t = lax.all_to_all(grads_above, "pipe", 0, 0)

    query_all = None
    key_parts = []
    value_parts = []
    for micro in range(micro_count):
        key_own_grad, value_own_grad, kv_back, query_all = layer_call(
            queries, kv_own, kv_halo, grad_t, prob, out, query_all, micro, blocks_per_kv
        )
        kv_next = from_behind(kv_back, "seq", -1)
        key_parts.append(key_own_grad + kv_next[0].astype(jnp.float32))
        value_parts.append(value_own_grad + kv_next[1].astype(jnp.float32))
    query_all = query_all[0]
    key_grads = jnp.concatenate(key_parts, axis=0).astype(jnp.bfloat16)
    value_grads = jnp.concatenate(value_parts, axis=0).astype(jnp.bfloat16)
    return (query_all[None], key_grads[None], value_grads[None])


def solution(mesh):
    placed = (
        P("pipe", None, "seq", None),
        P("pipe", None, "seq", None),
        P("pipe", None, "seq", None),
        P(None, "seq", None),
        P(),
    )
    return jax.shard_map(
        device_body,
        mesh=mesh,
        in_specs=placed,
        out_specs=(
            P("pipe", None, "seq", None),
            P("pipe", None, "seq", None),
            P("pipe", None, "seq", None),
        ),
        check_vma=False,
    )
```

```python
import functools

import jax
import jax.numpy as jnp
from jax import lax
from jax.experimental import pallas as pl
from jax.experimental.pallas import tpu as pltpu
from jax.sharding import PartitionSpec as P


DH = 128
WINDOW = 128
SCALE = DH ** (-0.5)
NT = (((1,), (1,)), ((), ()))
TN = (((0,), (0,)), ((), ()))


def from_behind(block, axis, distance):
    devices = range(lax.axis_size(axis))
    route = [(i - distance, i) for i in devices if i - distance in devices]
    return lax.ppermute(block, axis, route)


def head_core(q, k, v, g, allowed):
    scores = lax.dot_general(q, k, NT, preferred_element_type=jnp.float32) * SCALE
    masked = jnp.where(allowed, scores, -jnp.inf)
    row_max = jnp.max(masked, axis=-1, keepdims=True)
    weights = jnp.exp(masked - row_max)
    prob = weights / jnp.sum(weights, axis=-1, keepdims=True)
    prob_low = prob.astype(jnp.bfloat16)
    out = jnp.dot(prob_low, v, preferred_element_type=jnp.float32)
    grad_prob = lax.dot_general(g, v, NT, preferred_element_type=jnp.float32)
    grad_dot = jnp.sum(g.astype(jnp.float32) * out, axis=-1, keepdims=True)
    grad_score = (prob * (grad_prob - grad_dot)).astype(jnp.bfloat16)
    return prob_low, grad_score


def chain_kernel(x_ref, halo_ref, g0_ref, m_ref, *rest, first, count):
    if len(rest) == 3:
        prev_ref, o_ref, g_out_ref = rest
    else:
        prev_ref = None
        o_ref, g_out_ref = rest
    width = o_ref.shape[2]
    heads = width // DH
    halo_first = first + count - halo_ref.shape[0]
    allowed = m_ref[...] != 0
    if prev_ref is None:
        o_ref[o_ref.shape[0] - 1] = g0_ref[...]
    else:
        top = first + count - 1
        o_ref[top:] = prev_ref[top:]

    def step(i, g):
        layer = first + count - 1 - i
        local = layer - halo_first
        k = jnp.concatenate(
            [halo_ref[local, :, :DH], x_ref[layer, :, width:width + DH]], axis=0
        )
        v = jnp.concatenate(
            [halo_ref[local, :, DH:], x_ref[layer, :, width + DH:]], axis=0
        )
        outs = []
        for h in range(heads):
            cols = slice(h * DH, (h + 1) * DH)
            q = x_ref[layer, :, cols]
            gh = g[:, cols]
            _, grad_score = head_core(q, k, v, gh, allowed)
            dq = jnp.dot(grad_score, k, preferred_element_type=jnp.float32) * SCALE
            outs.append((gh.astype(jnp.float32) + dq).astype(jnp.bfloat16))
        g_new = jnp.concatenate(outs, axis=-1) if heads > 1 else outs[0]
        o_ref[layer - 1] = g_new
        return g_new

    g_out_ref[...] = lax.fori_loop(0, count, step, g0_ref[...], unroll=True)


def chain_call(sent, halo, grad_top, allowed_i32, first, count, prev=None, interpret=False):
    layers, rows, _ = sent.shape
    width = grad_top.shape[1]
    operands = [sent, halo, grad_top, allowed_i32]
    if prev is not None:
        operands.append(prev)
    return pl.pallas_call(
        functools.partial(chain_kernel, first=first, count=count),
        out_shape=(
            jax.ShapeDtypeStruct((layers, rows, width), jnp.bfloat16),
            jax.ShapeDtypeStruct((rows, width), jnp.bfloat16),
        ),
        interpret=interpret,
    )(*operands)


def pack_kernel(q_hbm, k_hbm, v_hbm, send_hbm, kv_hbm, sems, *, blocks_per_kv):
    micro_count = q_hbm.shape[1]
    total = send_hbm.shape[2]
    bw = total - 2 * DH
    blocks = send_hbm.shape[0] // micro_count
    copies = [
        pltpu.make_async_copy(k_hbm.at[0], kv_hbm.at[0, 0], sems.at[0]),
        pltpu.make_async_copy(v_hbm.at[0], kv_hbm.at[1, 0], sems.at[1]),
    ]
    for m in range(micro_count):
        for b in range(blocks):
            g = b // blocks_per_kv
            dst = send_hbm.at[m * blocks + b]
            parts = (
                (q_hbm.at[0, m, :, pl.ds(b * bw, bw)], dst.at[:, pl.ds(0, bw)]),
                (k_hbm.at[0, m, :, pl.ds(g * DH, DH)], dst.at[:, pl.ds(bw, DH)]),
                (v_hbm.at[0, m, :, pl.ds(g * DH, DH)], dst.at[:, pl.ds(bw + DH, DH)]),
            )
            for src, to in parts:
                copies.append(pltpu.make_async_copy(src, to, sems.at[len(copies)]))
    for c in copies:
        c.start()
    for c in copies:
        c.wait()


def pack_call(queries, keys, values, head_blocks, blocks_per_kv, interpret=False):
    _, micro_count, rows, width = queries.shape
    bw = width // head_blocks
    any_spec = pl.BlockSpec(memory_space=pl.ANY)
    return pl.pallas_call(
        functools.partial(pack_kernel, blocks_per_kv=blocks_per_kv),
        in_specs=[any_spec, any_spec, any_spec],
        out_specs=[any_spec, any_spec],
        out_shape=[
            jax.ShapeDtypeStruct((micro_count * head_blocks, rows, bw + 2 * DH), jnp.bfloat16),
            jax.ShapeDtypeStruct((2,) + keys.shape, jnp.bfloat16),
        ],
        scratch_shapes=[pltpu.SemaphoreType.DMA((2 + 3 * micro_count * head_blocks,))],
        interpret=interpret,
    )(queries, keys, values)


def layer_pre_kernel(q_ref, kvo_ref, kvh_ref, m_ref, p_ref, o_ref):
    heads = q_ref.shape[3] // DH
    allowed = m_ref[0] != 0
    k = jnp.concatenate([kvh_ref[0, 0, 0], kvo_ref[0, 0, 0]], axis=0)
    v = jnp.concatenate([kvh_ref[1, 0, 0], kvo_ref[1, 0, 0]], axis=0)
    for h in range(heads):
        q = q_ref[0, 0, :, h * DH:(h + 1) * DH]
        scores = lax.dot_general(q, k, NT, preferred_element_type=jnp.float32) * SCALE
        masked = jnp.where(allowed, scores, -jnp.inf)
        row_max = jnp.max(masked, axis=-1, keepdims=True)
        weights = jnp.exp(masked - row_max)
        prob = weights / jnp.sum(weights, axis=-1, keepdims=True)
        p_ref[0, h] = prob
        o_ref[0, h] = jnp.dot(prob.astype(jnp.bfloat16), v, preferred_element_type=jnp.float32)


def layer_pre_call(queries, kv_own, kv_halo, allowed_i32, interpret=False):
    _, micro_count, rows, width = queries.shape
    kv_heads = kv_own.shape[4] // DH
    group = width // (kv_heads * DH)
    kv_spec = pl.BlockSpec((2, 1, 1, rows, DH), lambda m, g: (0, 0, m, 0, g))
    return pl.pallas_call(
        layer_pre_kernel,
        grid=(micro_count, kv_heads),
        in_specs=[pl.BlockSpec((1, 1, rows, group * DH), lambda m, g: (0, m, 0, g)),
                  kv_spec, kv_spec,
                  pl.BlockSpec((1, rows, 2 * rows), lambda m, g: (m, 0, 0))],
        out_specs=[pl.BlockSpec((1, group, rows, 2 * rows), lambda m, g: (m, g, 0, 0)),
                   pl.BlockSpec((1, group, rows, DH), lambda m, g: (m, g, 0, 0))],
        out_shape=[
            jax.ShapeDtypeStruct((micro_count, kv_heads * group, rows, 2 * rows), jnp.float32),
            jax.ShapeDtypeStruct((micro_count, kv_heads * group, rows, DH), jnp.float32),
        ],
        interpret=interpret,
    )(queries, kv_own, kv_halo, allowed_i32)


def layer_kernel(q_ref, kvo_ref, kvh_ref, ga_ref, gb_ref, p_ref, o_ref, *rest):
    dk_ref, dv_ref, back_ref, gl_ref = rest[-4:]
    heads = q_ref.shape[3] // DH
    rows = q_ref.shape[2]
    k = jnp.concatenate([kvh_ref[0, 0, 0], kvo_ref[0, 0, 0]], axis=0)
    v = jnp.concatenate([kvh_ref[1, 0, 0], kvo_ref[1, 0, 0]], axis=0)
    grad = jnp.concatenate([ga_ref[0], gb_ref[0]], axis=-1)
    dk = None
    dv = None
    for h in range(heads):
        cols = slice(h * DH, (h + 1) * DH)
        q = q_ref[0, 0, :, cols]
        g = grad[:, cols]
        prob = p_ref[0, h]
        prob_low = prob.astype(jnp.bfloat16)
        grad_prob = lax.dot_general(g, v, NT, preferred_element_type=jnp.float32)
        grad_dot = jnp.sum(g.astype(jnp.float32) * o_ref[0, h], axis=-1, keepdims=True)
        grad_score = (prob * (grad_prob - grad_dot)).astype(jnp.bfloat16)
        dq = jnp.dot(grad_score, k, preferred_element_type=jnp.float32) * SCALE
        gl_ref[0, 0, :, cols] = (g.astype(jnp.float32) + dq).astype(jnp.bfloat16)
        dk_h = lax.dot_general(grad_score, q, TN, preferred_element_type=jnp.float32)
        dv_h = lax.dot_general(prob_low, g, TN, preferred_element_type=jnp.float32)
        dk = dk_h if dk is None else dk + dk_h
        dv = dv_h if dv is None else dv + dv_h
    dk = dk * SCALE
    back_ref[0, 0] = dk[:rows].astype(back_ref.dtype)
    back_ref[1, 0] = dv[:rows].astype(back_ref.dtype)
    dk_ref[0] = dk[rows:]
    dv_ref[0] = dv[rows:]


def layer_call(queries, kv_own, kv_halo, grad_t, prob, out, grad_prev, micro,
               blocks_per_kv, interpret=False):
    _, _, rows, width = queries.shape
    kv_heads = kv_own.shape[4] // DH
    group = width // (kv_heads * DH)
    gw = group * DH
    bw = grad_t.shape[2]
    kv_spec = pl.BlockSpec((2, 1, 1, rows, DH), lambda i, g: (0, 0, micro, 0, g))
    q_spec = pl.BlockSpec((1, 1, rows, gw), lambda i, g: (0, micro, 0, g))
    head_blocks = width // bw
    ga_spec = pl.BlockSpec(
        (1, rows, bw), lambda i, g: (micro * head_blocks + g * blocks_per_kv, 0, 0))
    gb_spec = pl.BlockSpec(
        (1, rows, bw), lambda i, g: (micro * head_blocks + g * blocks_per_kv + 1, 0, 0))
    p_spec = pl.BlockSpec((1, group, rows, 2 * rows), lambda i, g: (micro, g, 0, 0))
    o_spec = pl.BlockSpec((1, group, rows, DH), lambda i, g: (micro, g, 0, 0))
    own_out = pl.BlockSpec((1, rows, DH), lambda i, g: (0, 0, g))
    own_shape = jax.ShapeDtypeStruct((1, rows, kv_heads * DH), jnp.float32)
    in_specs = [q_spec, kv_spec, kv_spec, ga_spec, gb_spec, p_spec, o_spec]
    operands = [queries, kv_own, kv_halo, grad_t, grad_t, prob, out]
    aliases = {}
    if grad_prev is not None:
        in_specs.append(pl.BlockSpec(memory_space=pl.ANY))
        operands.append(grad_prev)
        aliases = {len(operands) - 1: 3}
    return pl.pallas_call(
        layer_kernel,
        grid=(1, kv_heads),
        in_specs=in_specs,
        out_specs=[own_out, own_out,
                   pl.BlockSpec((2, 1, rows, DH), lambda i, g: (0, 0, 0, g)),
                   q_spec],
        out_shape=[own_shape, own_shape,
                   jax.ShapeDtypeStruct((2, 1, rows, kv_heads * DH), jnp.bfloat16),
                   jax.ShapeDtypeStruct(queries.shape, jnp.bfloat16)],
        input_output_aliases=aliases,
        interpret=interpret,
    )(*operands)


def device_body(queries, keys, values, out_grad, segments):
    micro_count = queries.shape[1]
    row_count = queries.shape[2]
    query_width = queries.shape[3]
    key_width = keys.shape[3]
    section_count = lax.axis_size("pipe")
    section_index = lax.axis_index("pipe")
    seq_index = lax.axis_index("seq")
    kv_heads = key_width // DH
    q_heads = query_width // DH
    group_size = q_heads // kv_heads
    head_blocks = section_count // micro_count
    block_heads = q_heads // head_blocks
    block_width = block_heads * DH
    blocks_per_kv = group_size // block_heads
    send, kv_own = pack_call(queries, keys, values, head_blocks, blocks_per_kv)
    seg_padded = jnp.concatenate(
        [jnp.full((micro_count, row_count), -1, jnp.int32), segments], axis=1
    )
    query_pos = seq_index * row_count + jnp.arange(row_count, dtype=jnp.int32)
    key_pos = seq_index * row_count - row_count + jnp.arange(2 * row_count, dtype=jnp.int32)
    seg_query = lax.dynamic_slice_in_dim(
        seg_padded, seq_index * row_count + row_count, row_count, axis=1
    )
    seg_key = lax.dynamic_slice_in_dim(seg_padded, seq_index * row_count, 2 * row_count, axis=1)
    near = (
        (key_pos[None, :] <= query_pos[:, None])
        & (query_pos[:, None] - key_pos[None, :] < WINDOW)
        & (key_pos[None, :] >= 0)
    )
    masks = (near[None] & (seg_query[:, :, None] == seg_key[:, None, :])).astype(jnp.int32)
    kv_halo = from_behind(kv_own, "seq", 1)

    my_block = section_index % head_blocks
    my_micro = section_index // head_blocks
    sent = lax.all_to_all(send, "pipe", 0, 0)
    prob, out = layer_pre_call(queries, kv_own, kv_halo, masks)
    split_at = section_count // 2
    halo_hi = from_behind(sent[split_at:, :, block_width:], "seq", 1)
    halo_lo = from_behind(sent[1:split_at, :, block_width:], "seq", 1)
    grad_top = lax.dynamic_slice(
        out_grad, (my_micro, 0, my_block * block_width), (1, row_count, block_width)
    )[0]
    allowed = lax.dynamic_index_in_dim(masks, my_micro, 0, keepdims=False)
    above_hi, grad_mid = chain_call(
        sent, halo_hi, grad_top, allowed, split_at, section_count - split_at)
    grads_above, _ = chain_call(sent, halo_lo, grad_mid, allowed, 1, split_at - 1, above_hi)
    grad_t = lax.all_to_all(grads_above, "pipe", 0, 0)

    query_all = None
    key_parts = []
    value_parts = []
    for micro in range(micro_count):
        key_own_grad, value_own_grad, kv_back, query_all = layer_call(
            queries, kv_own, kv_halo, grad_t, prob, out, query_all, micro, blocks_per_kv
        )
        kv_next = from_behind(kv_back, "seq", -1)
        key_parts.append(key_own_grad + kv_next[0].astype(jnp.float32))
        value_parts.append(value_own_grad + kv_next[1].astype(jnp.float32))
    query_all = query_all[0]
    key_grads = jnp.concatenate(key_parts, axis=0).astype(jnp.bfloat16)
    value_grads = jnp.concatenate(value_parts, axis=0).astype(jnp.bfloat16)
    return (query_all[None], key_grads[None], value_grads[None])


def solution(mesh):
    placed = (
        P("pipe", None, "seq", None),
        P("pipe", None, "seq", None),
        P("pipe", None, "seq", None),
        P(None, "seq", None),
        P(),
    )
    return jax.shard_map(
        device_body,
        mesh=mesh,
        in_specs=placed,
        out_specs=(
            P("pipe", None, "seq", None),
            P("pipe", None, "seq", None),
            P("pipe", None, "seq", None),
        ),
        check_vma=False,
    )
```

```python
import functools

import jax
import jax.numpy as jnp
from jax import lax
from jax.experimental import pallas as pl
from jax.sharding import PartitionSpec as P


DH = 128
WINDOW = 128
SCALE = DH ** (-0.5)
NT = (((1,), (1,)), ((), ()))
TN = (((0,), (0,)), ((), ()))


def from_behind(block, axis, distance):
    devices = range(lax.axis_size(axis))
    route = [(i - distance, i) for i in devices if i - distance in devices]
    return lax.ppermute(block, axis, route)


def head_core(q, k, v, g, allowed):
    scores = lax.dot_general(q, k, NT, preferred_element_type=jnp.float32) * SCALE
    masked = jnp.where(allowed, scores, -jnp.inf)
    row_max = jnp.max(masked, axis=-1, keepdims=True)
    weights = jnp.exp(masked - row_max)
    prob = weights / jnp.sum(weights, axis=-1, keepdims=True)
    prob_low = prob.astype(jnp.bfloat16)
    out = jnp.dot(prob_low, v, preferred_element_type=jnp.float32)
    grad_prob = lax.dot_general(g, v, NT, preferred_element_type=jnp.float32)
    grad_dot = jnp.sum(g.astype(jnp.float32) * out, axis=-1, keepdims=True)
    grad_score = (prob * (grad_prob - grad_dot)).astype(jnp.bfloat16)
    return prob_low, grad_score


def chain_kernel(x_ref, halo_ref, g0_ref, m_ref, *rest, first, count, x_first):
    if len(rest) == 3:
        prev_ref, o_ref, g_out_ref = rest
    else:
        prev_ref = None
        o_ref, g_out_ref = rest
    width = o_ref.shape[2]
    heads = width // DH
    halo_first = first + count - halo_ref.shape[0]
    allowed = m_ref[...] != 0
    top = first + count - 1
    if prev_ref is None:
        o_ref[o_ref.shape[0] - 1] = g0_ref[...]
    else:
        o_ref[top] = g0_ref[...]
        o_ref[top + 1:] = prev_ref[top + 1 - (o_ref.shape[0] - prev_ref.shape[0]):]

    def step(i, g):
        layer = top - i
        local = layer - halo_first
        xl = layer - x_first
        k = jnp.concatenate(
            [halo_ref[local, :, :DH], x_ref[xl, :, width:width + DH]], axis=0
        )
        v = jnp.concatenate(
            [halo_ref[local, :, DH:], x_ref[xl, :, width + DH:]], axis=0
        )
        outs = []
        for h in range(heads):
            cols = slice(h * DH, (h + 1) * DH)
            q = x_ref[xl, :, cols]
            gh = g[:, cols]
            _, grad_score = head_core(q, k, v, gh, allowed)
            dq = jnp.dot(grad_score, k, preferred_element_type=jnp.float32) * SCALE
            outs.append((gh.astype(jnp.float32) + dq).astype(jnp.bfloat16))
        g_new = jnp.concatenate(outs, axis=-1) if heads > 1 else outs[0]
        o_ref[layer - 1] = g_new
        return g_new

    g_out_ref[...] = lax.fori_loop(0, count, step, g0_ref[...], unroll=True)


def chain_call(sent, halo, grad_top, allowed_i32, first, count, prev=None, interpret=False):
    layers, rows, total = sent.shape
    width = grad_top.shape[1]
    half = layers // 2
    x_block = (first + count - 1) // half
    x_spec = pl.BlockSpec((half, rows, total), lambda i: (x_block, 0, 0))
    operands = [sent, halo, grad_top, allowed_i32]
    full_specs = [pl.BlockSpec(a.shape, lambda i, n=a.ndim: (0,) * n) for a in operands[1:]]
    in_specs = [x_spec] + full_specs
    if prev is not None:
        operands.append(prev)
        in_specs.append(pl.BlockSpec((half, rows, width), lambda i: (1, 0, 0)))
    return pl.pallas_call(
        functools.partial(chain_kernel, first=first, count=count, x_first=x_block * half),
        in_specs=in_specs,
        grid=(1,),
        out_specs=(pl.BlockSpec((layers, rows, width), lambda i: (0, 0, 0)),
                   pl.BlockSpec((rows, width), lambda i: (0, 0))),
        out_shape=(
            jax.ShapeDtypeStruct((layers, rows, width), jnp.bfloat16),
            jax.ShapeDtypeStruct((rows, width), jnp.bfloat16),
        ),
        interpret=interpret,
    )(*operands)


def pack_kernel(q_ref, k_ref, v_ref, send_ref, kv_ref, *, blocks_per_kv):
    blocks, _, total = send_ref.shape
    bw = total - 2 * DH
    q = q_ref[0, 0]
    k = k_ref[0, 0]
    v = v_ref[0, 0]
    for b in range(blocks):
        g = b // blocks_per_kv
        send_ref[b, :, :bw] = q[:, b * bw:(b + 1) * bw]
        send_ref[b, :, bw:bw + DH] = k[:, g * DH:(g + 1) * DH]
        send_ref[b, :, bw + DH:] = v[:, g * DH:(g + 1) * DH]
    kv_ref[0, 0, 0] = k
    kv_ref[1, 0, 0] = v


def pack_call(queries, keys, values, head_blocks, blocks_per_kv, interpret=False):
    _, micro_count, rows, width = queries.shape
    key_width = keys.shape[3]
    bw = width // head_blocks
    kv_in = pl.BlockSpec((1, 1, rows, key_width), lambda m: (0, m, 0, 0))
    return pl.pallas_call(
        functools.partial(pack_kernel, blocks_per_kv=blocks_per_kv),
        grid=(micro_count,),
        in_specs=[pl.BlockSpec((1, 1, rows, width), lambda m: (0, m, 0, 0)), kv_in, kv_in],
        out_specs=[pl.BlockSpec((head_blocks, rows, bw + 2 * DH), lambda m: (m, 0, 0)),
                   pl.BlockSpec((2, 1, 1, rows, key_width), lambda m: (0, 0, m, 0, 0))],
        out_shape=[
            jax.ShapeDtypeStruct((micro_count * head_blocks, rows, bw + 2 * DH), jnp.bfloat16),
            jax.ShapeDtypeStruct((2,) + keys.shape, jnp.bfloat16),
        ],
        interpret=interpret,
    )(queries, keys, values)


def layer_pre_kernel(q_ref, kvo_ref, kvh_ref, m_ref, p_ref, o_ref):
    heads = q_ref.shape[3] // DH
    allowed = m_ref[0] != 0
    k = jnp.concatenate([kvh_ref[0, 0, 0], kvo_ref[0, 0, 0]], axis=0)
    v = jnp.concatenate([kvh_ref[1, 0, 0], kvo_ref[1, 0, 0]], axis=0)
    for h in range(heads):
        q = q_ref[0, 0, :, h * DH:(h + 1) * DH]
        scores = lax.dot_general(q, k, NT, preferred_element_type=jnp.float32) * SCALE
        masked = jnp.where(allowed, scores, -jnp.inf)
        row_max = jnp.max(masked, axis=-1, keepdims=True)
        weights = jnp.exp(masked - row_max)
        prob = weights / jnp.sum(weights, axis=-1, keepdims=True)
        p_ref[0, h] = prob
        o_ref[0, h] = jnp.dot(prob.astype(jnp.bfloat16), v, preferred_element_type=jnp.float32)


def layer_pre_call(queries, kv_own, kv_halo, allowed_i32, interpret=False):
    _, micro_count, rows, width = queries.shape
    kv_heads = kv_own.shape[4] // DH
    group = width // (kv_heads * DH)
    kv_spec = pl.BlockSpec((2, 1, 1, rows, DH), lambda m, g: (0, 0, m, 0, g))
    return pl.pallas_call(
        layer_pre_kernel,
        grid=(micro_count, kv_heads),
        in_specs=[pl.BlockSpec((1, 1, rows, group * DH), lambda m, g: (0, m, 0, g)),
                  kv_spec, kv_spec,
                  pl.BlockSpec((1, rows, 2 * rows), lambda m, g: (m, 0, 0))],
        out_specs=[pl.BlockSpec((1, group, rows, 2 * rows), lambda m, g: (m, g, 0, 0)),
                   pl.BlockSpec((1, group, rows, DH), lambda m, g: (m, g, 0, 0))],
        out_shape=[
            jax.ShapeDtypeStruct((micro_count, kv_heads * group, rows, 2 * rows), jnp.float32),
            jax.ShapeDtypeStruct((micro_count, kv_heads * group, rows, DH), jnp.float32),
        ],
        interpret=interpret,
    )(queries, kv_own, kv_halo, allowed_i32)


def layer_kernel(q_ref, kvo_ref, kvh_ref, ga_ref, gb_ref, p_ref, o_ref, *rest):
    dk_ref, dv_ref, back_ref, gl_ref = rest[-4:]
    heads = q_ref.shape[3] // DH
    rows = q_ref.shape[2]
    k = jnp.concatenate([kvh_ref[0, 0, 0], kvo_ref[0, 0, 0]], axis=0)
    v = jnp.concatenate([kvh_ref[1, 0, 0], kvo_ref[1, 0, 0]], axis=0)
    grad = jnp.concatenate([ga_ref[0], gb_ref[0]], axis=-1)
    dk = None
    dv = None
    for h in range(heads):
        cols = slice(h * DH, (h + 1) * DH)
        q = q_ref[0, 0, :, cols]
        g = grad[:, cols]
        prob = p_ref[0, h]
        prob_low = prob.astype(jnp.bfloat16)
        grad_prob = lax.dot_general(g, v, NT, preferred_element_type=jnp.float32)
        grad_dot = jnp.sum(g.astype(jnp.float32) * o_ref[0, h], axis=-1, keepdims=True)
        grad_score = (prob * (grad_prob - grad_dot)).astype(jnp.bfloat16)
        dq = jnp.dot(grad_score, k, preferred_element_type=jnp.float32) * SCALE
        gl_ref[0, 0, :, cols] = (g.astype(jnp.float32) + dq).astype(jnp.bfloat16)
        dk_h = lax.dot_general(grad_score, q, TN, preferred_element_type=jnp.float32)
        dv_h = lax.dot_general(prob_low, g, TN, preferred_element_type=jnp.float32)
        dk = dk_h if dk is None else dk + dk_h
        dv = dv_h if dv is None else dv + dv_h
    dk = dk * SCALE
    back_ref[0, 0] = dk[:rows].astype(back_ref.dtype)
    back_ref[1, 0] = dv[:rows].astype(back_ref.dtype)
    dk_ref[0] = dk[rows:]
    dv_ref[0] = dv[rows:]


def layer_call(queries, kv_own, kv_halo, grad_t, prob, out, grad_prev, micro,
               blocks_per_kv, interpret=False):
    _, _, rows, width = queries.shape
    kv_heads = kv_own.shape[4] // DH
    group = width // (kv_heads * DH)
    gw = group * DH
    bw = grad_t.shape[2]
    kv_spec = pl.BlockSpec((2, 1, 1, rows, DH), lambda i, g: (0, 0, micro, 0, g))
    q_spec = pl.BlockSpec((1, 1, rows, gw), lambda i, g: (0, micro, 0, g))
    head_blocks = width // bw
    ga_spec = pl.BlockSpec(
        (1, rows, bw), lambda i, g: (micro * head_blocks + g * blocks_per_kv, 0, 0))
    gb_spec = pl.BlockSpec(
        (1, rows, bw), lambda i, g: (micro * head_blocks + g * blocks_per_kv + 1, 0, 0))
    p_spec = pl.BlockSpec((1, group, rows, 2 * rows), lambda i, g: (micro, g, 0, 0))
    o_spec = pl.BlockSpec((1, group, rows, DH), lambda i, g: (micro, g, 0, 0))
    own_out = pl.BlockSpec((1, rows, DH), lambda i, g: (0, 0, g))
    own_shape = jax.ShapeDtypeStruct((1, rows, kv_heads * DH), jnp.float32)
    in_specs = [q_spec, kv_spec, kv_spec, ga_spec, gb_spec, p_spec, o_spec]
    operands = [queries, kv_own, kv_halo, grad_t, grad_t, prob, out]
    aliases = {}
    if grad_prev is not None:
        in_specs.append(pl.BlockSpec(memory_space=pl.ANY))
        operands.append(grad_prev)
        aliases = {len(operands) - 1: 3}
    return pl.pallas_call(
        layer_kernel,
        grid=(1, kv_heads),
        in_specs=in_specs,
        out_specs=[own_out, own_out,
                   pl.BlockSpec((2, 1, rows, DH), lambda i, g: (0, 0, 0, g)),
                   q_spec],
        out_shape=[own_shape, own_shape,
                   jax.ShapeDtypeStruct((2, 1, rows, kv_heads * DH), jnp.bfloat16),
                   jax.ShapeDtypeStruct(queries.shape, jnp.bfloat16)],
        input_output_aliases=aliases,
        interpret=interpret,
    )(*operands)


def device_body(queries, keys, values, out_grad, segments):
    micro_count = queries.shape[1]
    row_count = queries.shape[2]
    query_width = queries.shape[3]
    key_width = keys.shape[3]
    section_count = lax.axis_size("pipe")
    section_index = lax.axis_index("pipe")
    seq_index = lax.axis_index("seq")
    kv_heads = key_width // DH
    q_heads = query_width // DH
    group_size = q_heads // kv_heads
    head_blocks = section_count // micro_count
    block_heads = q_heads // head_blocks
    block_width = block_heads * DH
    blocks_per_kv = group_size // block_heads
    send, kv_own = pack_call(queries, keys, values, head_blocks, blocks_per_kv)
    seg_padded = jnp.concatenate(
        [jnp.full((micro_count, row_count), -1, jnp.int32), segments], axis=1
    )
    query_pos = seq_index * row_count + jnp.arange(row_count, dtype=jnp.int32)
    key_pos = seq_index * row_count - row_count + jnp.arange(2 * row_count, dtype=jnp.int32)
    seg_query = lax.dynamic_slice_in_dim(
        seg_padded, seq_index * row_count + row_count, row_count, axis=1
    )
    seg_key = lax.dynamic_slice_in_dim(seg_padded, seq_index * row_count, 2 * row_count, axis=1)
    near = (
        (key_pos[None, :] <= query_pos[:, None])
        & (query_pos[:, None] - key_pos[None, :] < WINDOW)
        & (key_pos[None, :] >= 0)
    )
    masks = (near[None] & (seg_query[:, :, None] == seg_key[:, None, :])).astype(jnp.int32)
    kv_halo = from_behind(kv_own, "seq", 1)

    my_block = section_index % head_blocks
    my_micro = section_index // head_blocks
    sent = lax.all_to_all(send, "pipe", 0, 0)
    prob, out = layer_pre_call(queries, kv_own, kv_halo, masks)
    split_at = section_count // 2
    halo_hi = from_behind(sent[split_at:, :, block_width:], "seq", 1)
    halo_lo = from_behind(sent[1:split_at, :, block_width:], "seq", 1)
    grad_top = lax.dynamic_slice(
        out_grad, (my_micro, 0, my_block * block_width), (1, row_count, block_width)
    )[0]
    allowed = lax.dynamic_index_in_dim(masks, my_micro, 0, keepdims=False)
    above_hi, grad_mid = chain_call(
        sent, halo_hi, grad_top, allowed, split_at, section_count - split_at)
    grads_above, _ = chain_call(sent, halo_lo, grad_mid, allowed, 1, split_at - 1, above_hi)
    grad_t = lax.all_to_all(grads_above, "pipe", 0, 0)

    query_all = None
    key_parts = []
    value_parts = []
    for micro in range(micro_count):
        key_own_grad, value_own_grad, kv_back, query_all = layer_call(
            queries, kv_own, kv_halo, grad_t, prob, out, query_all, micro, blocks_per_kv
        )
        kv_next = from_behind(kv_back, "seq", -1)
        key_parts.append(key_own_grad + kv_next[0].astype(jnp.float32))
        value_parts.append(value_own_grad + kv_next[1].astype(jnp.float32))
    query_all = query_all[0]
    key_grads = jnp.concatenate(key_parts, axis=0).astype(jnp.bfloat16)
    value_grads = jnp.concatenate(value_parts, axis=0).astype(jnp.bfloat16)
    return (query_all[None], key_grads[None], value_grads[None])


def solution(mesh):
    placed = (
        P("pipe", None, "seq", None),
        P("pipe", None, "seq", None),
        P("pipe", None, "seq", None),
        P(None, "seq", None),
        P(),
    )
    return jax.shard_map(
        device_body,
        mesh=mesh,
        in_specs=placed,
        out_specs=(
            P("pipe", None, "seq", None),
            P("pipe", None, "seq", None),
            P("pipe", None, "seq", None),
        ),
        check_vma=False,
    )
```

```python
import functools

import jax
import jax.numpy as jnp
from jax import lax
from jax.experimental import pallas as pl
from jax.sharding import PartitionSpec as P


DH = 128
WINDOW = 128
SCALE = DH ** (-0.5)
NT = (((1,), (1,)), ((), ()))
TN = (((0,), (0,)), ((), ()))


def from_behind(block, axis, distance):
    devices = range(lax.axis_size(axis))
    route = [(i - distance, i) for i in devices if i - distance in devices]
    return lax.ppermute(block, axis, route)


def head_core(q, k, v, g, allowed):
    scores = lax.dot_general(q, k, NT, preferred_element_type=jnp.float32) * SCALE
    masked = jnp.where(allowed, scores, -jnp.inf)
    row_max = jnp.max(masked, axis=-1, keepdims=True)
    weights = jnp.exp(masked - row_max)
    prob = weights / jnp.sum(weights, axis=-1, keepdims=True)
    prob_low = prob.astype(jnp.bfloat16)
    out = jnp.dot(prob_low, v, preferred_element_type=jnp.float32)
    grad_prob = lax.dot_general(g, v, NT, preferred_element_type=jnp.float32)
    grad_dot = jnp.sum(g.astype(jnp.float32) * out, axis=-1, keepdims=True)
    grad_score = (prob * (grad_prob - grad_dot)).astype(jnp.bfloat16)
    return prob_low, grad_score


def chain_kernel(x_ref, halo_ref, g0_ref, m_ref, *rest, first, count, x_first):
    if len(rest) == 3:
        prev_ref, o_ref, g_out_ref = rest
    else:
        prev_ref = None
        o_ref, g_out_ref = rest
    width = o_ref.shape[2]
    heads = width // DH
    halo_first = first + count - halo_ref.shape[0]
    allowed = m_ref[...] != 0
    top = first + count - 1
    if prev_ref is None:
        o_ref[o_ref.shape[0] - 1] = g0_ref[...]
    else:
        o_ref[top] = g0_ref[...]
        o_ref[top + 1:] = prev_ref[top + 1 - (o_ref.shape[0] - prev_ref.shape[0]):]

    def step(i, g):
        layer = top - i
        local = layer - halo_first
        xl = layer - x_first
        k = jnp.concatenate(
            [halo_ref[local, :, :DH], x_ref[xl, :, width:width + DH]], axis=0
        )
        v = jnp.concatenate(
            [halo_ref[local, :, DH:], x_ref[xl, :, width + DH:]], axis=0
        )
        outs = []
        for h in range(heads):
            cols = slice(h * DH, (h + 1) * DH)
            q = x_ref[xl, :, cols]
            gh = g[:, cols]
            _, grad_score = head_core(q, k, v, gh, allowed)
            dq = jnp.dot(grad_score, k, preferred_element_type=jnp.float32) * SCALE
            outs.append((gh.astype(jnp.float32) + dq).astype(jnp.bfloat16))
        g_new = jnp.concatenate(outs, axis=-1) if heads > 1 else outs[0]
        o_ref[layer - 1] = g_new
        return g_new

    g_out_ref[...] = lax.fori_loop(0, count, step, g0_ref[...], unroll=True)


def chain_call(sent, halo, grad_top, allowed_i32, first, count, prev=None, interpret=False):
    layers, rows, total = sent.shape
    width = grad_top.shape[1]
    half = layers // 2
    x_block = (first + count - 1) // half
    x_spec = pl.BlockSpec((half, rows, total), lambda i: (x_block, 0, 0))
    operands = [sent, halo, grad_top, allowed_i32]
    full_specs = [pl.BlockSpec(a.shape, lambda i, n=a.ndim: (0,) * n) for a in operands[1:]]
    in_specs = [x_spec] + full_specs
    if prev is not None:
        operands.append(prev)
        in_specs.append(pl.BlockSpec((half, rows, width), lambda i: (1, 0, 0)))
    return pl.pallas_call(
        functools.partial(chain_kernel, first=first, count=count, x_first=x_block * half),
        in_specs=in_specs,
        grid=(1,),
        out_specs=(pl.BlockSpec((layers, rows, width), lambda i: (0, 0, 0)),
                   pl.BlockSpec((rows, width), lambda i: (0, 0))),
        out_shape=(
            jax.ShapeDtypeStruct((layers, rows, width), jnp.bfloat16),
            jax.ShapeDtypeStruct((rows, width), jnp.bfloat16),
        ),
        interpret=interpret,
    )(*operands)


def pack_kernel(q_ref, k_ref, v_ref, send_ref, kv_ref, *, blocks_per_kv):
    blocks, _, total = send_ref.shape
    bw = total - 2 * DH
    q = q_ref[0, 0]
    k = k_ref[0, 0]
    v = v_ref[0, 0]
    for b in range(blocks):
        g = b // blocks_per_kv
        send_ref[b, :, :bw] = q[:, b * bw:(b + 1) * bw]
        send_ref[b, :, bw:bw + DH] = k[:, g * DH:(g + 1) * DH]
        send_ref[b, :, bw + DH:] = v[:, g * DH:(g + 1) * DH]
    kv_ref[0, 0, 0] = k
    kv_ref[1, 0, 0] = v


def pack_call(queries, keys, values, head_blocks, blocks_per_kv, interpret=False):
    _, micro_count, rows, width = queries.shape
    key_width = keys.shape[3]
    bw = width // head_blocks
    kv_in = pl.BlockSpec((1, 1, rows, key_width), lambda m: (0, m, 0, 0))
    return pl.pallas_call(
        functools.partial(pack_kernel, blocks_per_kv=blocks_per_kv),
        grid=(micro_count,),
        in_specs=[pl.BlockSpec((1, 1, rows, width), lambda m: (0, m, 0, 0)), kv_in, kv_in],
        out_specs=[pl.BlockSpec((head_blocks, rows, bw + 2 * DH), lambda m: (m, 0, 0)),
                   pl.BlockSpec((2, 1, 1, rows, key_width), lambda m: (0, 0, m, 0, 0))],
        out_shape=[
            jax.ShapeDtypeStruct((micro_count * head_blocks, rows, bw + 2 * DH), jnp.bfloat16),
            jax.ShapeDtypeStruct((2,) + keys.shape, jnp.bfloat16),
        ],
        interpret=interpret,
    )(queries, keys, values)


def layer_pre_kernel(q_ref, kvo_ref, kvh_ref, m_ref, p_ref, o_ref):
    heads = q_ref.shape[3] // DH
    allowed = m_ref[0] != 0
    k = jnp.concatenate([kvh_ref[0, 0, 0], kvo_ref[0, 0, 0]], axis=0)
    v = jnp.concatenate([kvh_ref[1, 0, 0], kvo_ref[1, 0, 0]], axis=0)
    for h in range(heads):
        q = q_ref[0, 0, :, h * DH:(h + 1) * DH]
        scores = lax.dot_general(q, k, NT, preferred_element_type=jnp.float32) * SCALE
        masked = jnp.where(allowed, scores, -jnp.inf)
        row_max = jnp.max(masked, axis=-1, keepdims=True)
        weights = jnp.exp(masked - row_max)
        prob = weights / jnp.sum(weights, axis=-1, keepdims=True)
        p_ref[0, h] = prob
        o_ref[0, h] = jnp.dot(prob.astype(jnp.bfloat16), v, preferred_element_type=jnp.float32)


def layer_pre_call(queries, kv_own, kv_halo, allowed_i32, interpret=False):
    _, micro_count, rows, width = queries.shape
    kv_heads = kv_own.shape[4] // DH
    group = width // (kv_heads * DH)
    kv_spec = pl.BlockSpec((2, 1, 1, rows, DH), lambda m, g: (0, 0, m, 0, g))
    return pl.pallas_call(
        layer_pre_kernel,
        grid=(micro_count, kv_heads),
        in_specs=[pl.BlockSpec((1, 1, rows, group * DH), lambda m, g: (0, m, 0, g)),
                  kv_spec, kv_spec,
                  pl.BlockSpec((1, rows, 2 * rows), lambda m, g: (m, 0, 0))],
        out_specs=[pl.BlockSpec((1, group, rows, 2 * rows), lambda m, g: (m, g, 0, 0)),
                   pl.BlockSpec((1, group, rows, DH), lambda m, g: (m, g, 0, 0))],
        out_shape=[
            jax.ShapeDtypeStruct((micro_count, kv_heads * group, rows, 2 * rows), jnp.float32),
            jax.ShapeDtypeStruct((micro_count, kv_heads * group, rows, DH), jnp.float32),
        ],
        interpret=interpret,
    )(queries, kv_own, kv_halo, allowed_i32)


def layer_kernel(q_ref, kvo_ref, kvh_ref, g_ref, p_ref, o_ref, *rest):
    dk_ref, dv_ref, back_ref, gl_ref = rest[-4:]
    pairs = kvo_ref.shape[4] // DH
    heads = q_ref.shape[3] // (DH * pairs)
    rows = q_ref.shape[2]
    grad = jnp.concatenate([g_ref[j] for j in range(g_ref.shape[0])], axis=-1)
    for c in range(pairs):
        kc = slice(c * DH, (c + 1) * DH)
        layer_group(q_ref, kvo_ref, kvh_ref, grad, p_ref, o_ref, dk_ref, dv_ref, back_ref,
                    gl_ref, c, kc, heads, rows)


def layer_group(q_ref, kvo_ref, kvh_ref, grad, p_ref, o_ref, dk_ref, dv_ref, back_ref,
                gl_ref, c, kc, heads, rows):
    k = jnp.concatenate([kvh_ref[0, 0, 0, :, kc], kvo_ref[0, 0, 0, :, kc]], axis=0)
    v = jnp.concatenate([kvh_ref[1, 0, 0, :, kc], kvo_ref[1, 0, 0, :, kc]], axis=0)
    dk = None
    dv = None
    for hh in range(heads):
        h = c * heads + hh
        cols = slice(h * DH, (h + 1) * DH)
        q = q_ref[0, 0, :, cols]
        g = grad[:, cols]
        prob = p_ref[0, h]
        prob_low = prob.astype(jnp.bfloat16)
        grad_prob = lax.dot_general(g, v, NT, preferred_element_type=jnp.float32)
        grad_dot = jnp.sum(g.astype(jnp.float32) * o_ref[0, h], axis=-1, keepdims=True)
        grad_score = (prob * (grad_prob - grad_dot)).astype(jnp.bfloat16)
        dq = jnp.dot(grad_score, k, preferred_element_type=jnp.float32) * SCALE
        gl_ref[0, 0, :, cols] = (g.astype(jnp.float32) + dq).astype(jnp.bfloat16)
        dk_h = lax.dot_general(grad_score, q, TN, preferred_element_type=jnp.float32)
        dv_h = lax.dot_general(prob_low, g, TN, preferred_element_type=jnp.float32)
        dk = dk_h if dk is None else dk + dk_h
        dv = dv_h if dv is None else dv + dv_h
    dk = dk * SCALE
    back_ref[0, 0, :, kc] = dk[:rows].astype(back_ref.dtype)
    back_ref[1, 0, :, kc] = dv[:rows].astype(back_ref.dtype)
    dk_ref[0, :, kc] = dk[rows:]
    dv_ref[0, :, kc] = dv[rows:]


def layer_call(queries, kv_own, kv_halo, grad_t, prob, out, grad_prev, micro,
               blocks_per_kv, interpret=False):
    _, _, rows, width = queries.shape
    kv_heads = kv_own.shape[4] // DH
    group = width // (kv_heads * DH)
    gw = group * DH
    bw = grad_t.shape[2]
    pairs = 2
    kv_spec = pl.BlockSpec((2, 1, 1, rows, pairs * DH), lambda i, g: (0, 0, micro, 0, g))
    q_spec = pl.BlockSpec((1, 1, rows, pairs * gw), lambda i, g: (0, micro, 0, g))
    steps = kv_heads // pairs
    g_spec = pl.BlockSpec(
        (pairs * blocks_per_kv, rows, bw), lambda i, g: (micro * steps + g, 0, 0))
    p_spec = pl.BlockSpec((1, pairs * group, rows, 2 * rows), lambda i, g: (micro, g, 0, 0))
    o_spec = pl.BlockSpec((1, pairs * group, rows, DH), lambda i, g: (micro, g, 0, 0))
    own_out = pl.BlockSpec((1, rows, pairs * DH), lambda i, g: (0, 0, g))
    own_shape = jax.ShapeDtypeStruct((1, rows, kv_heads * DH), jnp.float32)
    in_specs = [q_spec, kv_spec, kv_spec, g_spec, p_spec, o_spec]
    operands = [queries, kv_own, kv_halo, grad_t, prob, out]
    aliases = {}
    if grad_prev is not None:
        in_specs.append(pl.BlockSpec(memory_space=pl.ANY))
        operands.append(grad_prev)
        aliases = {len(operands) - 1: 3}
    return pl.pallas_call(
        layer_kernel,
        grid=(1, steps),
        in_specs=in_specs,
        out_specs=[own_out, own_out,
                   pl.BlockSpec((2, 1, rows, pairs * DH), lambda i, g: (0, 0, 0, g)),
                   q_spec],
        out_shape=[own_shape, own_shape,
                   jax.ShapeDtypeStruct((2, 1, rows, kv_heads * DH), jnp.bfloat16),
                   jax.ShapeDtypeStruct(queries.shape, jnp.bfloat16)],
        input_output_aliases=aliases,
        interpret=interpret,
    )(*operands)


def device_body(queries, keys, values, out_grad, segments):
    micro_count = queries.shape[1]
    row_count = queries.shape[2]
    query_width = queries.shape[3]
    key_width = keys.shape[3]
    section_count = lax.axis_size("pipe")
    section_index = lax.axis_index("pipe")
    seq_index = lax.axis_index("seq")
    kv_heads = key_width // DH
    q_heads = query_width // DH
    group_size = q_heads // kv_heads
    head_blocks = section_count // micro_count
    block_heads = q_heads // head_blocks
    block_width = block_heads * DH
    blocks_per_kv = group_size // block_heads
    send, kv_own = pack_call(queries, keys, values, head_blocks, blocks_per_kv)
    seg_padded = jnp.concatenate(
        [jnp.full((micro_count, row_count), -1, jnp.int32), segments], axis=1
    )
    query_pos = seq_index * row_count + jnp.arange(row_count, dtype=jnp.int32)
    key_pos = seq_index * row_count - row_count + jnp.arange(2 * row_count, dtype=jnp.int32)
    seg_query = lax.dynamic_slice_in_dim(
        seg_padded, seq_index * row_count + row_count, row_count, axis=1
    )
    seg_key = lax.dynamic_slice_in_dim(seg_padded, seq_index * row_count, 2 * row_count, axis=1)
    near = (
        (key_pos[None, :] <= query_pos[:, None])
        & (query_pos[:, None] - key_pos[None, :] < WINDOW)
        & (key_pos[None, :] >= 0)
    )
    masks = (near[None] & (seg_query[:, :, None] == seg_key[:, None, :])).astype(jnp.int32)
    kv_halo = from_behind(kv_own, "seq", 1)

    my_block = section_index % head_blocks
    my_micro = section_index // head_blocks
    sent = lax.all_to_all(send, "pipe", 0, 0)
    prob, out = layer_pre_call(queries, kv_own, kv_halo, masks)
    split_at = section_count // 2
    halo_hi = from_behind(sent[split_at:, :, block_width:], "seq", 1)
    halo_lo = from_behind(sent[1:split_at, :, block_width:], "seq", 1)
    grad_top = lax.dynamic_slice(
        out_grad, (my_micro, 0, my_block * block_width), (1, row_count, block_width)
    )[0]
    allowed = lax.dynamic_index_in_dim(masks, my_micro, 0, keepdims=False)
    above_hi, grad_mid = chain_call(
        sent, halo_hi, grad_top, allowed, split_at, section_count - split_at)
    grads_above, _ = chain_call(sent, halo_lo, grad_mid, allowed, 1, split_at - 1, above_hi)
    grad_t = lax.all_to_all(grads_above, "pipe", 0, 0)

    query_all = None
    key_parts = []
    value_parts = []
    for micro in range(micro_count):
        key_own_grad, value_own_grad, kv_back, query_all = layer_call(
            queries, kv_own, kv_halo, grad_t, prob, out, query_all, micro, blocks_per_kv
        )
        kv_next = from_behind(kv_back, "seq", -1)
        key_parts.append(key_own_grad + kv_next[0].astype(jnp.float32))
        value_parts.append(value_own_grad + kv_next[1].astype(jnp.float32))
    query_all = query_all[0]
    key_grads = jnp.concatenate(key_parts, axis=0).astype(jnp.bfloat16)
    value_grads = jnp.concatenate(value_parts, axis=0).astype(jnp.bfloat16)
    return (query_all[None], key_grads[None], value_grads[None])


def solution(mesh):
    placed = (
        P("pipe", None, "seq", None),
        P("pipe", None, "seq", None),
        P("pipe", None, "seq", None),
        P(None, "seq", None),
        P(),
    )
    return jax.shard_map(
        device_body,
        mesh=mesh,
        in_specs=placed,
        out_specs=(
            P("pipe", None, "seq", None),
            P("pipe", None, "seq", None),
            P("pipe", None, "seq", None),
        ),
        check_vma=False,
    )
```
